256 devices in a mesh: gy: 8 (over z), gx: 32 (over y, x, core).
Axes of the slice: x: 4, y: 4, z: 8, core: 2. Of those that a mesh axis runs over, the one named last changes fastest.
Arguments:
- saved_thickness: bfloat16 [2, 512, 8192], P(None, 'gy', 'gx'), may hold values from 0.5 to 2
- saved_velocity: bfloat16 [2, 2, 512, 8192], P(None, None, 'gy', 'gx'), may hold values from -4 to 4
- surface_slope: bfloat16 [2, 512, 8192], P(None, 'gy', 'gx'), may hold values from -3 to 3
- basal_beta: float32 [512, 8192], P('gy', 'gx'), may hold values from 0.2 to 5
- cell_mask: int32 [512, 8192], P('gy', 'gx'), may hold values from 0 to 2
- upwind_flags: int32 [512, 8192], P('gy', 'gx'), may hold values from 0 to 3
- observed_velocity: bfloat16 [2, 2, 512, 8192], P(None, None, 'gy', 'gx'), may hold values from -60 to 60
- thickness_adjoint: float32 [512, 8192], P('gy', 'gx'), may hold values from -6 to 6
Outputs:
- beta_gradient: float32 [512, 8192], P('gy', 'gx')
- thickness_gradient: float32 [512, 8192], P('gy', 'gx')
- misfit: float32 [], replicated
The draws below stay inside these ranges and needn't reach their ends.
All inputs are finite; a program needn't handle non-finite values.
Results may differ from the reference program's by a relative error of at most 0.0003.
Values sent between devices are 32-bit elements; how exact they have to be, the bound alone decides.
No kernel may reach another device: no remote copies, remote signals or barrier semaphores. Data moves between devices by JAX's collectives and lax.ppermute only.
A program may use at most 64 MiB of HBM per device.

```python
import math
import jax
import jax.numpy as jnp
from jax import lax

SWEEPS = 3
STEPS = 2
NY = 512
NX = 8192


def draw_observed_velocity(key, part):
    row_ramp = 1.0 + 2.0 * jnp.arange(NY, dtype=jnp.float32) / NY
    col_ramp = 1.0 + 2.0 * jnp.arange(NX, dtype=jnp.float32) / NX
    ramp_field = row_ramp[:, None] * col_ramp[None, :]
    noise = jnp.clip(jax.random.normal(key, (STEPS, 2, NY, NX), jnp.float32), -4.0, 4.0)
    return (noise * ramp_field[None, None]).astype(jnp.bfloat16)


def place_ends(drawn, own_key, smallest, high):
    place = [jax.random.randint(jax.random.fold_in(own_key, axis), (), 0, length) for axis, length in enumerate(drawn.shape)]
    main_axis = drawn.shape.index(max(drawn.shape))
    beside = place[:main_axis] + [(place[main_axis] + 1) % drawn.shape[main_axis]] + place[main_axis + 1:]
    return drawn.at[tuple(place)].set(smallest).at[tuple(beside)].set(high)


def block_scale(own_key, extent, cuts, least, high):
    def one(axis_at, blocks):
        heights = jax.random.uniform(jax.random.fold_in(jax.random.fold_in(own_key, 6), axis_at), (blocks,), jnp.float32, least / len(cuts), high / len(cuts))
        return jnp.repeat(jnp.exp(heights), extent[axis_at] // blocks).reshape((-1,) + (1,) * (len(extent) - axis_at - 1))

    factor_of = one(*cuts[0])
    for cut in cuts[1:]:
        factor_of = factor_of * one(*cut)
    return factor_of


def gaussian(rng, extent, width, most, split=(), kind=jnp.bfloat16):
    array = width * jax.random.normal(rng, extent, jnp.float32)
    if split:
        array = array * block_scale(rng, extent, split, -0.22, 0.18)
    return jnp.clip(array, -most, most).astype(kind)


def setup_inputs(seed: int = 0) -> dict:
    splits = jax.random.split(jax.random.key(seed), 9)
    return {
        "saved_thickness": jnp.clip(0.5 + 1.5 * jax.random.uniform(splits[0], (STEPS, NY, NX), jnp.float32) ** block_scale(splits[0], (STEPS, NY, NX), ((1, 8), (2, 32)), -0.2, 0.2), 0.5, 2.0).astype(jnp.bfloat16),
        "saved_velocity": gaussian(splits[1], (STEPS, 2, NY, NX), 1.0, 4.0, ((2, 8), (3, 32))),
        "surface_slope": gaussian(splits[2], (2, NY, NX), 0.5, 3.0, ((1, 8), (2, 32))),
        "basal_beta": jnp.clip(jnp.exp(math.log(5.0) - 3.218876 * jax.random.uniform(splits[3], (NY, NX), jnp.float32) ** block_scale(splits[3], (NY, NX), ((0, 8), (1, 32)), -0.2, 0.2)), 0.2, 5.0),
        "cell_mask": place_ends(jax.random.randint(splits[4], (NY, NX), 0, 3), jax.random.fold_in(splits[4], 1), 0, 2).astype(jnp.int32),
        "upwind_flags": place_ends(jax.random.randint(splits[5], (NY, NX), 0, 4), jax.random.fold_in(splits[5], 1), 0, 3).astype(jnp.int32),
        "observed_velocity": draw_observed_velocity(jax.random.fold_in(splits[8], 71), 0),
        "thickness_adjoint": gaussian(splits[7], (NY, NX), 1.0, 6.0, ((0, 8), (1, 32)), jnp.float32),
    }


RELAXATION = 0.8
TIME_STEP = 0.1
EPSILON = 1e-06
OFFSETS = ((0, 1), (2, 1), (1, 0), (1, 2))

def shifted(padded, row_offset, col_offset):
    row_count = padded.shape[-2] - 2
    col_count = padded.shape[-1] - 2
    return padded[..., row_offset:row_offset + row_count, col_offset:col_offset + col_count]

def sweep_core(velocity_pad, thick_pad, cover_pad, friction, forcing):
    center = shifted(velocity_pad, 1, 1)
    thick_mid = shifted(thick_pad, 1, 1)
    cover_mid = shifted(cover_pad, 1, 1)
    flux_sum = jnp.zeros_like(center)
    coupling_sum = jnp.zeros_like(thick_mid)
    for row_offset, col_offset in OFFSETS:
        difference = shifted(velocity_pad, row_offset, col_offset) - center
        strain = lax.optimization_barrier(jnp.sum(difference * difference, axis=0))
        coupling = 0.5 * (thick_mid + shifted(thick_pad, row_offset, col_offset)) * cover_mid * shifted(cover_pad, row_offset, col_offset) * jnp.power(1.0 + strain, -1.0 / 3.0)
        flux_sum = flux_sum + coupling * difference
        coupling_sum = coupling_sum + coupling
    residual = forcing - friction * center + flux_sum
    return cover_mid * (center + RELAXATION * residual / (1.0 + friction + coupling_sum))

def transport_core(thick_pad, velocity_pad, cover_pad, donor_east_pad, donor_south_pad):
    east_cover = cover_pad[1:-1, :-1] * cover_pad[1:-1, 1:]
    speed_east = 0.5 * (velocity_pad[0, 1:-1, :-1] + velocity_pad[0, 1:-1, 1:])
    donor_east = donor_east_pad[1:-1, :-1]
    flux_east = speed_east * east_cover * (donor_east * thick_pad[1:-1, :-1] + (1.0 - donor_east) * thick_pad[1:-1, 1:])
    south_cover = cover_pad[:-1, 1:-1] * cover_pad[1:, 1:-1]
    speed_south = 0.5 * (velocity_pad[1, :-1, 1:-1] + velocity_pad[1, 1:, 1:-1])
    donor_south = donor_south_pad[:-1, 1:-1]
    flux_south = speed_south * south_cover * (donor_south * thick_pad[:-1, 1:-1] + (1.0 - donor_south) * thick_pad[1:, 1:-1])
    diverge = flux_east[:, 1:] - flux_east[:, :-1] + flux_south[1:, :] - flux_south[:-1, :]
    return cover_pad[1:-1, 1:-1] * (thick_pad[1:-1, 1:-1] - TIME_STEP * diverge)

def pad_one(values):
    widths = [(0, 0)] * (values.ndim - 2) + [(1, 1), (1, 1)]
    return jnp.pad(values, widths)

def forward_step(thickness, friction, initial_guess, slope_field, cover_pad, donor_east_pad, donor_south_pad):
    forcing = thickness * slope_field
    thick_pad = pad_one(thickness)
    velocity = initial_guess
    sweep_step = jax.checkpoint(sweep_core)
    for sweep_index in range(SWEEPS):
        velocity = sweep_step(pad_one(velocity), thick_pad, cover_pad, friction, forcing)
    thick_next = jax.checkpoint(transport_core)(thick_pad, pad_one(velocity), cover_pad, donor_east_pad, donor_south_pad)
    return (velocity, thick_next)

def reference(saved_thickness, saved_velocity, surface_slope, basal_beta, cell_mask, upwind_flags, observed_velocity, thickness_adjoint):
    cover = (cell_mask > 0).astype(jnp.float32)
    grounded = (cell_mask == 2).astype(jnp.float32)
    friction = basal_beta * grounded
    slope_field = surface_slope.astype(jnp.float32)
    cover_pad = pad_one(cover)
    donor_east_pad = pad_one((upwind_flags % 2).astype(jnp.float32))
    donor_south_pad = pad_one((upwind_flags // 2).astype(jnp.float32))
    cotangent = thickness_adjoint
    beta_gradient = jnp.zeros_like(basal_beta)
    misfit = jnp.zeros((), jnp.float32)
    for step_index in reversed(range(STEPS)):
        initial_guess = saved_velocity[step_index].astype(jnp.float32)
        observed = observed_velocity[step_index].astype(jnp.float32)
        misfit_scale = jnp.mean(grounded * lax.optimization_barrier(jnp.sum(observed * observed, axis=0))) + EPSILON

        def advance(thickness, friction_field):
            return forward_step(thickness, friction_field, initial_guess, slope_field, cover_pad, donor_east_pad, donor_south_pad)
        (velocity, thick_next), pullback = jax.vjp(advance, saved_thickness[step_index].astype(jnp.float32), friction)
        difference = velocity - observed
        misfit_field = grounded * difference
        misfit = misfit + 0.5 * jnp.mean(lax.optimization_barrier(jnp.sum(misfit_field * difference, axis=0))) / misfit_scale
        cotangent, friction_bar = pullback((misfit_field / misfit_scale, cotangent))
        beta_gradient = beta_gradient + grounded * friction_bar
    return (beta_gradient, cotangent, misfit)
```

```python
import jax
import jax.numpy as jnp
from jax import lax
from jax.sharding import PartitionSpec as P

SWEEPS = 3


RELAXATION = 0.8
TIME_STEP = 0.1
EPSILON = 1e-06
OFFSETS = ((0, 1), (2, 1), (1, 0), (1, 2))
HALO = 11


def padded_2(block, sides, width):
    for axis, dim in sides:
        count = lax.axis_size(axis)
        forward = [(i, i + 1) for i in range(count - 1)]
        backward = [(target, source) for source, target in forward]
        low = lax.ppermute(
            lax.slice_in_dim(block, block.shape[dim] - width, None, axis=dim), axis, forward
        )
        high = lax.ppermute(lax.slice_in_dim(block, 0, width, axis=dim), axis, backward)
        block = jnp.concatenate([low, block, high], axis=dim)
    return block


def shifted(padded, row_offset, col_offset):
    row_count = padded.shape[-2] - 2
    col_count = padded.shape[-1] - 2
    return padded[..., row_offset : row_offset + row_count, col_offset : col_offset + col_count]


def pad_one(values):
    widths = [(0, 0)] * (values.ndim - 2) + [(1, 1), (1, 1)]
    return jnp.pad(values, widths)


def sweep_core(velocity_pad, thick_pad, cover_pad, friction, forcing):
    center = shifted(velocity_pad, 1, 1)
    thick_mid = shifted(thick_pad, 1, 1)
    cover_mid = shifted(cover_pad, 1, 1)
    flux_sum = jnp.zeros_like(center)
    coupling_sum = jnp.zeros_like(thick_mid)
    for row_offset, col_offset in OFFSETS:
        difference = shifted(velocity_pad, row_offset, col_offset) - center
        strain = jnp.sum(difference * difference, axis=0)
        coupling = (
            0.5
            * (thick_mid + shifted(thick_pad, row_offset, col_offset))
            * cover_mid
            * shifted(cover_pad, row_offset, col_offset)
            * jnp.power(1.0 + strain, -1.0 / 3.0)
        )
        flux_sum = flux_sum + coupling * difference
        coupling_sum = coupling_sum + coupling
    residual = forcing - friction * center + flux_sum
    return cover_mid * (center + RELAXATION * residual / (1.0 + friction + coupling_sum))


def transport_core(thick_pad, velocity_pad, cover_pad, donor_east_pad, donor_south_pad):
    east_cover = cover_pad[1:-1, :-1] * cover_pad[1:-1, 1:]
    speed_east = 0.5 * (velocity_pad[0, 1:-1, :-1] + velocity_pad[0, 1:-1, 1:])
    donor_east = donor_east_pad[1:-1, :-1]
    flux_east = (
        speed_east
        * east_cover
        * (donor_east * thick_pad[1:-1, :-1] + (1.0 - donor_east) * thick_pad[1:-1, 1:])
    )
    south_cover = cover_pad[:-1, 1:-1] * cover_pad[1:, 1:-1]
    speed_south = 0.5 * (velocity_pad[1, :-1, 1:-1] + velocity_pad[1, 1:, 1:-1])
    donor_south = donor_south_pad[:-1, 1:-1]
    flux_south = (
        speed_south
        * south_cover
        * (donor_south * thick_pad[:-1, 1:-1] + (1.0 - donor_south) * thick_pad[1:, 1:-1])
    )
    diverge = flux_east[:, 1:] - flux_east[:, :-1] + flux_south[1:, :] - flux_south[:-1, :]
    return cover_pad[1:-1, 1:-1] * (thick_pad[1:-1, 1:-1] - TIME_STEP * diverge)


def forward_step(thickness, friction, initial_guess, slope_field, cover_pad, donor_east_pad, donor_south_pad):
    forcing = thickness * slope_field
    thick_pad = pad_one(thickness)
    velocity = initial_guess
    for sweep_index in range(SWEEPS):
        velocity = sweep_core(pad_one(velocity), thick_pad, cover_pad, friction, forcing)
    thick_next = transport_core(thick_pad, pad_one(velocity), cover_pad, donor_east_pad, donor_south_pad)
    return (velocity, thick_next)


def on_device(
    saved_thickness,
    saved_velocity,
    surface_slope,
    basal_beta,
    cell_mask,
    upwind_flags,
    observed_velocity,
    thickness_adjoint,
):
    steps = saved_thickness.shape[0]
    rows, cols = basal_beta.shape
    f32 = jnp.float32
    fields = jnp.concatenate(
        [
            jnp.stack([cell_mask.astype(f32), upwind_flags.astype(f32), basal_beta]),
            surface_slope.astype(f32),
            saved_thickness.astype(f32),
            saved_velocity.astype(f32).reshape(steps * 2, rows, cols),
            observed_velocity.astype(f32).reshape(steps * 2, rows, cols),
            thickness_adjoint[None],
        ],
        axis=0,
    )
    wide = padded_2(fields, (("gy", 1), ("gx", 2)), HALO)
    mask = wide[0].astype(jnp.int32)
    flags = wide[1].astype(jnp.int32)
    cover = (mask > 0).astype(f32)
    grounded = (mask == 2).astype(f32)
    friction = wide[2] * grounded
    slope_field = wide[3:5]
    thick_all = wide[5 : 5 + steps]
    vel_all = wide[5 + steps : 5 + 3 * steps].reshape(steps, 2, *wide.shape[1:])
    obs_all = wide[5 + 3 * steps : 5 + 5 * steps].reshape(steps, 2, *wide.shape[1:])
    cotangent = wide[5 + 5 * steps]
    cover_pad = pad_one(cover)
    donor_east_pad = pad_one((flags % 2).astype(f32))
    donor_south_pad = pad_one((flags // 2).astype(f32))

    def centre(values):
        return values[..., HALO : HALO + rows, HALO : HALO + cols]

    grounded_c = centre(grounded)
    cell_count = rows * cols * lax.axis_size("gy") * lax.axis_size("gx")
    pullbacks = {}
    seeds = {}
    local_sums = []
    for step_index in reversed(range(steps)):
        initial_guess = vel_all[step_index]
        observed = obs_all[step_index]

        def advance(thickness, friction_field, initial_guess=initial_guess):
            return forward_step(
                thickness, friction_field, initial_guess, slope_field, cover_pad, donor_east_pad, donor_south_pad
            )

        (velocity, unused_next), pullback = jax.vjp(advance, thick_all[step_index], friction)
        difference = velocity - observed
        misfit_field = grounded * difference
        pullbacks[step_index] = pullback
        seeds[step_index] = misfit_field
        local_sums.append(0.5 * jnp.sum(centre(misfit_field * difference)))
        obs_c = centre(observed)
        local_sums.append(jnp.sum(grounded_c * jnp.sum(obs_c * obs_c, axis=0)))
    totals = lax.psum(jnp.stack(local_sums), ("gy", "gx"))
    beta_gradient = jnp.zeros_like(friction)
    misfit = jnp.zeros((), f32)
    for k, step_index in enumerate(reversed(range(steps))):
        misfit_scale = totals[2 * k + 1] / cell_count + EPSILON
        misfit = misfit + totals[2 * k] / cell_count / misfit_scale
        cotangent, friction_bar = pullbacks[step_index]((seeds[step_index] / misfit_scale, cotangent))
        beta_gradient = beta_gradient + grounded * friction_bar
    return (centre(beta_gradient), centre(cotangent), misfit)


def solution(mesh):
    in_specs = (
        P(None, "gy", "gx"),
        P(None, None, "gy", "gx"),
        P(None, "gy", "gx"),
        P("gy", "gx"),
        P("gy", "gx"),
        P("gy", "gx"),
        P(None, None, "gy", "gx"),
        P("gy", "gx"),
    )
    out_specs = (P("gy", "gx"), P("gy", "gx"), P())
    return jax.shard_map(
        on_device, mesh=mesh, in_specs=in_specs, out_specs=out_specs, check_vma=False
    )
```

```python
import jax
import jax.numpy as jnp
from jax import lax
from jax.sharding import PartitionSpec as P

SWEEPS = 3


RELAXATION = 0.8
TIME_STEP = 0.1
EPSILON = 1e-06
OFFSETS = ((0, 1), (2, 1), (1, 0), (1, 2))
HALO = 11


def padded_2(block, sides, width):
    for axis, dim in sides:
        count = lax.axis_size(axis)
        forward = [(i, i + 1) for i in range(count - 1)]
        backward = [(target, source) for source, target in forward]
        low = lax.ppermute(
            lax.slice_in_dim(block, block.shape[dim] - width, None, axis=dim), axis, forward
        )
        high = lax.ppermute(lax.slice_in_dim(block, 0, width, axis=dim), axis, backward)
        block = jnp.concatenate([low, block, high], axis=dim)
    return block


def butterfly_sum(values, axes):
    for axis in axes:
        count = lax.axis_size(axis)
        if count & (count - 1):
            values = lax.psum(values, axis)
            continue
        stride = 1
        while stride < count:
            values = values + lax.ppermute(values, axis, [(i, i ^ stride) for i in range(count)])
            stride *= 2
    return values


def shifted(padded, row_offset, col_offset):
    row_count = padded.shape[-2] - 2
    col_count = padded.shape[-1] - 2
    return padded[..., row_offset : row_offset + row_count, col_offset : col_offset + col_count]


def pad_one(values):
    widths = [(0, 0)] * (values.ndim - 2) + [(1, 1), (1, 1)]
    return jnp.pad(values, widths)


def sweep_core(velocity_pad, thick_pad, cover_pad, friction, forcing):
    center = shifted(velocity_pad, 1, 1)
    thick_mid = shifted(thick_pad, 1, 1)
    cover_mid = shifted(cover_pad, 1, 1)
    flux_sum = jnp.zeros_like(center)
    coupling_sum = jnp.zeros_like(thick_mid)
    for row_offset, col_offset in OFFSETS:
        difference = shifted(velocity_pad, row_offset, col_offset) - center
        strain = jnp.sum(difference * difference, axis=0)
        coupling = (
            0.5
            * (thick_mid + shifted(thick_pad, row_offset, col_offset))
            * cover_mid
            * shifted(cover_pad, row_offset, col_offset)
            * jnp.power(1.0 + strain, -1.0 / 3.0)
        )
        flux_sum = flux_sum + coupling * difference
        coupling_sum = coupling_sum + coupling
    residual = forcing - friction * center + flux_sum
    return cover_mid * (center + RELAXATION * residual / (1.0 + friction + coupling_sum))


def transport_core(thick_pad, velocity_pad, cover_pad, donor_east_pad, donor_south_pad):
    east_cover = cover_pad[1:-1, :-1] * cover_pad[1:-1, 1:]
    speed_east = 0.5 * (velocity_pad[0, 1:-1, :-1] + velocity_pad[0, 1:-1, 1:])
    donor_east = donor_east_pad[1:-1, :-1]
    flux_east = (
        speed_east
        * east_cover
        * (donor_east * thick_pad[1:-1, :-1] + (1.0 - donor_east) * thick_pad[1:-1, 1:])
    )
    south_cover = cover_pad[:-1, 1:-1] * cover_pad[1:, 1:-1]
    speed_south = 0.5 * (velocity_pad[1, :-1, 1:-1] + velocity_pad[1, 1:, 1:-1])
    donor_south = donor_south_pad[:-1, 1:-1]
    flux_south = (
        speed_south
        * south_cover
        * (donor_south * thick_pad[:-1, 1:-1] + (1.0 - donor_south) * thick_pad[1:, 1:-1])
    )
    diverge = flux_east[:, 1:] - flux_east[:, :-1] + flux_south[1:, :] - flux_south[:-1, :]
    return cover_pad[1:-1, 1:-1] * (thick_pad[1:-1, 1:-1] - TIME_STEP * diverge)


def forward_step(thickness, friction, initial_guess, slope_field, cover_pad, donor_east_pad, donor_south_pad):
    forcing = thickness * slope_field
    thick_pad = pad_one(thickness)
    velocity = initial_guess
    for sweep_index in range(SWEEPS):
        velocity = sweep_core(pad_one(velocity), thick_pad, cover_pad, friction, forcing)
    thick_next = transport_core(thick_pad, pad_one(velocity), cover_pad, donor_east_pad, donor_south_pad)
    return (velocity, thick_next)


def on_device(
    saved_thickness,
    saved_velocity,
    surface_slope,
    basal_beta,
    cell_mask,
    upwind_flags,
    observed_velocity,
    thickness_adjoint,
):
    steps = saved_thickness.shape[0]
    rows, cols = basal_beta.shape
    f32 = jnp.float32
    fields = jnp.concatenate(
        [
            jnp.stack([cell_mask.astype(f32), upwind_flags.astype(f32), basal_beta]),
            surface_slope.astype(f32),
            saved_thickness.astype(f32),
            saved_velocity.astype(f32).reshape(steps * 2, rows, cols),
            observed_velocity.astype(f32).reshape(steps * 2, rows, cols),
            thickness_adjoint[None],
        ],
        axis=0,
    )
    wide = padded_2(fields, (("gy", 1), ("gx", 2)), HALO)
    mask = wide[0].astype(jnp.int32)
    flags = wide[1].astype(jnp.int32)
    cover = (mask > 0).astype(f32)
    grounded = (mask == 2).astype(f32)
    friction = wide[2] * grounded
    slope_field = wide[3:5]
    thick_all = wide[5 : 5 + steps]
    vel_all = wide[5 + steps : 5 + 3 * steps].reshape(steps, 2, *wide.shape[1:])
    obs_all = wide[5 + 3 * steps : 5 + 5 * steps].reshape(steps, 2, *wide.shape[1:])
    cotangent = wide[5 + 5 * steps]
    cover_pad = pad_one(cover)
    donor_east_pad = pad_one((flags % 2).astype(f32))
    donor_south_pad = pad_one((flags // 2).astype(f32))

    def centre(values):
        return values[..., HALO : HALO + rows, HALO : HALO + cols]

    grounded_c = centre(grounded)
    cell_count = rows * cols * lax.axis_size("gy") * lax.axis_size("gx")
    scale_local = []
    for step_index in range(steps):
        obs_c = centre(obs_all[step_index])
        scale_local.append(jnp.sum(grounded_c * jnp.sum(obs_c * obs_c, axis=0)))
    scale_totals = butterfly_sum(jnp.stack(scale_local), ("gx", "gy"))
    pullbacks = {}
    seeds = {}
    misfit_local = []
    for step_index in reversed(range(steps)):
        initial_guess = vel_all[step_index]
        observed = obs_all[step_index]

        def advance(thickness, friction_field, initial_guess=initial_guess):
            return forward_step(
                thickness, friction_field, initial_guess, slope_field, cover_pad, donor_east_pad, donor_south_pad
            )

        (velocity, unused_next), pullback = jax.vjp(advance, thick_all[step_index], friction)
        difference = velocity - observed
        misfit_field = grounded * difference
        pullbacks[step_index] = pullback
        seeds[step_index] = misfit_field
        misfit_local.append(0.5 * jnp.sum(centre(misfit_field * difference)))
    misfit_totals = butterfly_sum(jnp.stack(misfit_local), ("gx", "gy"))
    beta_gradient = jnp.zeros_like(friction)
    misfit = jnp.zeros((), f32)
    for k, step_index in enumerate(reversed(range(steps))):
        misfit_scale = scale_totals[step_index] / cell_count + EPSILON
        misfit = misfit + misfit_totals[k] / cell_count / misfit_scale
        cotangent, friction_bar = pullbacks[step_index]((seeds[step_index] / misfit_scale, cotangent))
        beta_gradient = beta_gradient + grounded * friction_bar
    return (centre(beta_gradient), centre(cotangent), misfit)


def solution(mesh):
    in_specs = (
        P(None, "gy", "gx"),
        P(None, None, "gy", "gx"),
        P(None, "gy", "gx"),
        P("gy", "gx"),
        P("gy", "gx"),
        P("gy", "gx"),
        P(None, None, "gy", "gx"),
        P("gy", "gx"),
    )
    out_specs = (P("gy", "gx"), P("gy", "gx"), P())
    return jax.shard_map(
        on_device, mesh=mesh, in_specs=in_specs, out_specs=out_specs, check_vma=False
    )
```

```python
import jax
import jax.numpy as jnp
from jax import lax
from jax.sharding import PartitionSpec as P


SWEEPS = 3


RELAXATION = 0.8
TIME_STEP = 0.1
EPSILON = 1e-06
OFFSETS = ((0, 1), (2, 1), (1, 0), (1, 2))
HALO = 11


def padded_2(block, sides, width):
    for axis, dim in sides:
        count = lax.axis_size(axis)
        forward = [(i, i + 1) for i in range(count - 1)]
        backward = [(target, source) for source, target in forward]
        low = lax.ppermute(
            lax.slice_in_dim(block, block.shape[dim] - width, None, axis=dim), axis, forward
        )
        high = lax.ppermute(lax.slice_in_dim(block, 0, width, axis=dim), axis, backward)
        block = jnp.concatenate([low, block, high], axis=dim)
    return block


def butterfly_sum(values, axes):
    for axis in axes:
        count = lax.axis_size(axis)
        if count & (count - 1):
            values = lax.psum(values, axis)
            continue
        stride = 1
        while stride < count:
            values = values + lax.ppermute(values, axis, [(i, i ^ stride) for i in range(count)])
            stride *= 2
    return values


def shifted(padded, row_offset, col_offset):
    row_count = padded.shape[-2] - 2
    col_count = padded.shape[-1] - 2
    return padded[..., row_offset : row_offset + row_count, col_offset : col_offset + col_count]


def pad_one(values):
    widths = [(0, 0)] * (values.ndim - 2) + [(1, 1), (1, 1)]
    return jnp.pad(values, widths)


def sweep_core(velocity_pad, thick_pad, cover_pad, friction, forcing):
    center = shifted(velocity_pad, 1, 1)
    thick_mid = shifted(thick_pad, 1, 1)
    cover_mid = shifted(cover_pad, 1, 1)
    flux_sum = jnp.zeros_like(center)
    coupling_sum = jnp.zeros_like(thick_mid)
    for row_offset, col_offset in OFFSETS:
        difference = shifted(velocity_pad, row_offset, col_offset) - center
        strain = jnp.sum(difference * difference, axis=0)
        coupling = (
            0.5
            * (thick_mid + shifted(thick_pad, row_offset, col_offset))
            * cover_mid
            * shifted(cover_pad, row_offset, col_offset)
            * jnp.power(1.0 + strain, -1.0 / 3.0)
        )
        flux_sum = flux_sum + coupling * difference
        coupling_sum = coupling_sum + coupling
    residual = forcing - friction * center + flux_sum
    return cover_mid * (center + RELAXATION * residual / (1.0 + friction + coupling_sum))


def transport_core(thick_pad, velocity_pad, cover_pad, donor_east_pad, donor_south_pad):
    east_cover = cover_pad[1:-1, :-1] * cover_pad[1:-1, 1:]
    speed_east = 0.5 * (velocity_pad[0, 1:-1, :-1] + velocity_pad[0, 1:-1, 1:])
    donor_east = donor_east_pad[1:-1, :-1]
    flux_east = (
        speed_east
        * east_cover
        * (donor_east * thick_pad[1:-1, :-1] + (1.0 - donor_east) * thick_pad[1:-1, 1:])
    )
    south_cover = cover_pad[:-1, 1:-1] * cover_pad[1:, 1:-1]
    speed_south = 0.5 * (velocity_pad[1, :-1, 1:-1] + velocity_pad[1, 1:, 1:-1])
    donor_south = donor_south_pad[:-1, 1:-1]
    flux_south = (
        speed_south
        * south_cover
        * (donor_south * thick_pad[:-1, 1:-1] + (1.0 - donor_south) * thick_pad[1:, 1:-1])
    )
    diverge = flux_east[:, 1:] - flux_east[:, :-1] + flux_south[1:, :] - flux_south[:-1, :]
    return cover_pad[1:-1, 1:-1] * (thick_pad[1:-1, 1:-1] - TIME_STEP * diverge)


def forward_step(thickness, friction, initial_guess, slope_field, cover_pad, donor_east_pad, donor_south_pad):
    forcing = thickness * slope_field
    thick_pad = pad_one(thickness)
    velocity = initial_guess
    for _ in range(SWEEPS):
        velocity = sweep_core(pad_one(velocity), thick_pad, cover_pad, friction, forcing)
    thick_next = transport_core(thick_pad, pad_one(velocity), cover_pad, donor_east_pad, donor_south_pad)
    return (velocity, thick_next)


def on_device_body(
    saved_thickness,
    saved_velocity,
    surface_slope,
    basal_beta,
    cell_mask,
    upwind_flags,
    observed_velocity,
    thickness_adjoint,
):
    steps = saved_thickness.shape[0]
    rows, cols = basal_beta.shape
    f32 = jnp.float32
    fields = jnp.concatenate(
        [
            jnp.stack([cell_mask.astype(f32), upwind_flags.astype(f32), basal_beta]),
            surface_slope.astype(f32),
            saved_thickness.astype(f32),
            saved_velocity.astype(f32).reshape(steps * 2, rows, cols),
            observed_velocity.astype(f32).reshape(steps * 2, rows, cols),
            thickness_adjoint[None],
        ],
        axis=0,
    )
    wide = padded_2(fields, (("gy", 1), ("gx", 2)), HALO)
    mask = wide[0].astype(jnp.int32)
    flags = wide[1].astype(jnp.int32)
    cover = (mask > 0).astype(f32)
    grounded = (mask == 2).astype(f32)
    friction = wide[2] * grounded
    slope_field = wide[3:5]
    thick_all = wide[5 : 5 + steps]
    vel_all = wide[5 + steps : 5 + 3 * steps].reshape(steps, 2, *wide.shape[1:])
    obs_all = wide[5 + 3 * steps : 5 + 5 * steps].reshape(steps, 2, *wide.shape[1:])
    cotangent = wide[5 + 5 * steps]
    cover_pad = pad_one(cover)
    donor_east_pad = pad_one((flags % 2).astype(f32))
    donor_south_pad = pad_one((flags // 2).astype(f32))

    def centre(values):
        return values[..., HALO : HALO + rows, HALO : HALO + cols]

    grounded_c = centre(grounded)
    cell_count = rows * cols * lax.axis_size("gy") * lax.axis_size("gx")
    obs_local, mask_local = lax.optimization_barrier(
        (observed_velocity.astype(f32), cell_mask)
    )
    grounded_local = (mask_local == 2).astype(f32)
    scale_local = [
        jnp.sum(grounded_local * jnp.sum(obs_local[n] * obs_local[n], axis=0)) for n in range(steps)
    ]
    scale_totals = butterfly_sum(jnp.stack(scale_local), ("gx", "gy"))
    pullbacks = {}
    seeds = {}
    misfit_local = []
    for step_index in reversed(range(steps)):
        initial_guess = vel_all[step_index]
        observed = obs_all[step_index]

        def advance(thickness, friction_field, initial_guess=initial_guess):
            return forward_step(
                thickness, friction_field, initial_guess, slope_field, cover_pad, donor_east_pad, donor_south_pad
            )

        (velocity, unused_next), pullback = jax.vjp(advance, thick_all[step_index], friction)
        difference = velocity - observed
        misfit_field = grounded * difference
        pullbacks[step_index] = pullback
        seeds[step_index] = misfit_field
        velocity_c, observed_c = lax.optimization_barrier((centre(velocity), centre(observed)))
        difference_c = velocity_c - observed_c
        misfit_local.append(0.5 * jnp.sum(grounded_c * difference_c * difference_c))
    misfit_totals = butterfly_sum(jnp.stack(misfit_local), ("gx", "gy"))
    beta_gradient = jnp.zeros_like(friction)
    misfit = jnp.zeros((), f32)
    for k, step_index in enumerate(reversed(range(steps))):
        misfit_scale = scale_totals[step_index] / cell_count + EPSILON
        misfit = misfit + misfit_totals[k] / cell_count / misfit_scale
        cotangent, friction_bar = pullbacks[step_index]((seeds[step_index] / misfit_scale, cotangent))
        beta_gradient = beta_gradient + grounded * friction_bar
    return (centre(beta_gradient), centre(cotangent), misfit)


def solution(mesh):
    in_specs = (
        P(None, "gy", "gx"),
        P(None, None, "gy", "gx"),
        P(None, "gy", "gx"),
        P("gy", "gx"),
        P("gy", "gx"),
        P("gy", "gx"),
        P(None, None, "gy", "gx"),
        P("gy", "gx"),
    )
    out_specs = (P("gy", "gx"), P("gy", "gx"), P())
    return jax.shard_map(on_device_body, mesh=mesh, in_specs=in_specs, out_specs=out_specs, check_vma=False)
```

```python
import jax
import jax.numpy as jnp
from jax import lax
from jax.sharding import PartitionSpec as P


SWEEPS = 3


RELAXATION = 0.8
TIME_STEP = 0.1
EPSILON = 1e-06
OFFSETS = ((0, 1), (2, 1), (1, 0), (1, 2))
HALO = 11


def padded_2(block, sides, width):
    for axis, dim in sides:
        count = lax.axis_size(axis)
        forward = [(i, i + 1) for i in range(count - 1)]
        backward = [(target, source) for source, target in forward]
        low = lax.ppermute(
            lax.slice_in_dim(block, block.shape[dim] - width, None, axis=dim), axis, forward
        )
        high = lax.ppermute(lax.slice_in_dim(block, 0, width, axis=dim), axis, backward)
        block = jnp.concatenate([low, block, high], axis=dim)
    return block


def butterfly_sum(values, axes):
    for axis in axes:
        count = lax.axis_size(axis)
        if count & (count - 1):
            values = lax.psum(values, axis)
            continue
        stride = 1
        while stride < count:
            values = values + lax.ppermute(values, axis, [(i, i ^ stride) for i in range(count)])
            stride *= 2
    return values


def shifted(padded, row_offset, col_offset):
    row_count = padded.shape[-2] - 2
    col_count = padded.shape[-1] - 2
    return padded[..., row_offset : row_offset + row_count, col_offset : col_offset + col_count]


def pad_one(values):
    widths = [(0, 0)] * (values.ndim - 2) + [(1, 1), (1, 1)]
    return jnp.pad(values, widths)


def sweep_core(velocity_pad, thick_pad, cover_pad, friction, forcing):
    center = shifted(velocity_pad, 1, 1)
    thick_mid = shifted(thick_pad, 1, 1)
    cover_mid = shifted(cover_pad, 1, 1)
    flux_sum = jnp.zeros_like(center)
    coupling_sum = jnp.zeros_like(thick_mid)
    for row_offset, col_offset in OFFSETS:
        difference = shifted(velocity_pad, row_offset, col_offset) - center
        strain = jnp.sum(difference * difference, axis=0)
        coupling = (
            0.5
            * (thick_mid + shifted(thick_pad, row_offset, col_offset))
            * cover_mid
            * shifted(cover_pad, row_offset, col_offset)
            * jnp.power(1.0 + strain, -1.0 / 3.0)
        )
        flux_sum = flux_sum + coupling * difference
        coupling_sum = coupling_sum + coupling
    residual = forcing - friction * center + flux_sum
    return cover_mid * (center + RELAXATION * residual / (1.0 + friction + coupling_sum))


def transport_core(thick_pad, velocity_pad, cover_pad, donor_east_pad, donor_south_pad):
    east_cover = cover_pad[1:-1, :-1] * cover_pad[1:-1, 1:]
    speed_east = 0.5 * (velocity_pad[0, 1:-1, :-1] + velocity_pad[0, 1:-1, 1:])
    donor_east = donor_east_pad[1:-1, :-1]
    flux_east = (
        speed_east
        * east_cover
        * (donor_east * thick_pad[1:-1, :-1] + (1.0 - donor_east) * thick_pad[1:-1, 1:])
    )
    south_cover = cover_pad[:-1, 1:-1] * cover_pad[1:, 1:-1]
    speed_south = 0.5 * (velocity_pad[1, :-1, 1:-1] + velocity_pad[1, 1:, 1:-1])
    donor_south = donor_south_pad[:-1, 1:-1]
    flux_south = (
        speed_south
        * south_cover
        * (donor_south * thick_pad[:-1, 1:-1] + (1.0 - donor_south) * thick_pad[1:, 1:-1])
    )
    diverge = flux_east[:, 1:] - flux_east[:, :-1] + flux_south[1:, :] - flux_south[:-1, :]
    return cover_pad[1:-1, 1:-1] * (thick_pad[1:-1, 1:-1] - TIME_STEP * diverge)


def forward_step(thickness, friction, initial_guess, slope_field, cover_pad, donor_east_pad, donor_south_pad):
    forcing = thickness * slope_field
    thick_pad = pad_one(thickness)
    velocity = initial_guess
    for _ in range(SWEEPS):
        velocity = sweep_core(pad_one(velocity), thick_pad, cover_pad, friction, forcing)
    thick_next = transport_core(thick_pad, pad_one(velocity), cover_pad, donor_east_pad, donor_south_pad)
    return (velocity, thick_next)


def on_device_body(
    saved_thickness,
    saved_velocity,
    surface_slope,
    basal_beta,
    cell_mask,
    upwind_flags,
    observed_velocity,
    thickness_adjoint,
):
    steps = saved_thickness.shape[0]
    rows, cols = basal_beta.shape
    f32 = jnp.float32
    fields = jnp.concatenate(
        [
            jnp.stack([cell_mask.astype(f32), upwind_flags.astype(f32), basal_beta]),
            surface_slope.astype(f32),
            saved_thickness.astype(f32),
            saved_velocity.astype(f32).reshape(steps * 2, rows, cols),
            observed_velocity.astype(f32).reshape(steps * 2, rows, cols),
            thickness_adjoint[None],
        ],
        axis=0,
    )
    wide = padded_2(fields, (("gy", 1), ("gx", 2)), HALO)
    mask = wide[0].astype(jnp.int32)
    flags = wide[1].astype(jnp.int32)
    cover = (mask > 0).astype(f32)
    grounded = (mask == 2).astype(f32)
    friction = wide[2] * grounded
    slope_field = wide[3:5]
    thick_all = wide[5 : 5 + steps]
    vel_all = wide[5 + steps : 5 + 3 * steps].reshape(steps, 2, *wide.shape[1:])
    obs_all = wide[5 + 3 * steps : 5 + 5 * steps].reshape(steps, 2, *wide.shape[1:])
    cotangent = wide[5 + 5 * steps]
    cover_pad = pad_one(cover)
    donor_east_pad = pad_one((flags % 2).astype(f32))
    donor_south_pad = pad_one((flags // 2).astype(f32))

    def centre(values):
        return values[..., HALO : HALO + rows, HALO : HALO + cols]

    grounded_c = centre(grounded)
    cell_count = rows * cols * lax.axis_size("gy") * lax.axis_size("gx")
    obs_local, mask_local = lax.optimization_barrier(
        (observed_velocity.astype(f32), cell_mask)
    )
    grounded_local = (mask_local == 2).astype(f32)
    scale_local = [
        jnp.sum(grounded_local * jnp.sum(obs_local[n] * obs_local[n], axis=0)) for n in range(steps)
    ]
    pullbacks = {}
    seeds = {}
    misfit_local = []
    for step_index in reversed(range(steps)):
        initial_guess = vel_all[step_index]
        observed = obs_all[step_index]

        def advance(thickness, friction_field, initial_guess=initial_guess):
            return forward_step(
                thickness, friction_field, initial_guess, slope_field, cover_pad, donor_east_pad, donor_south_pad
            )

        (velocity, unused_next), pullback = jax.vjp(advance, thick_all[step_index], friction)
        difference = velocity - observed
        misfit_field = grounded * difference
        pullbacks[step_index] = pullback
        seeds[step_index] = misfit_field
        velocity_c, observed_c = lax.optimization_barrier((centre(velocity), centre(observed)))
        difference_c = velocity_c - observed_c
        misfit_local.append(0.5 * jnp.sum(grounded_c * difference_c * difference_c))
    totals = butterfly_sum(jnp.stack(scale_local + misfit_local), ("gx", "gy"))
    last = steps - 1
    zero_seed = jnp.zeros_like(seeds[last])
    thick_a, friction_a = pullbacks[last]((seeds[last], jnp.zeros_like(cotangent)))
    thick_b, friction_b = pullbacks[last]((zero_seed, cotangent))
    beta_gradient = jnp.zeros_like(friction)
    misfit = jnp.zeros((), f32)
    for k, step_index in enumerate(reversed(range(steps))):
        misfit_scale = totals[step_index] / cell_count + EPSILON
        misfit = misfit + totals[steps + k] / cell_count / misfit_scale
        if step_index == last:
            cotangent = thick_a / misfit_scale + thick_b
            friction_bar = friction_a / misfit_scale + friction_b
        else:
            cotangent, friction_bar = pullbacks[step_index]((seeds[step_index] / misfit_scale, cotangent))
        beta_gradient = beta_gradient + grounded * friction_bar
    return (centre(beta_gradient), centre(cotangent), misfit)


def solution(mesh):
    in_specs = (
        P(None, "gy", "gx"),
        P(None, None, "gy", "gx"),
        P(None, "gy", "gx"),
        P("gy", "gx"),
        P("gy", "gx"),
        P("gy", "gx"),
        P(None, None, "gy", "gx"),
        P("gy", "gx"),
    )
    out_specs = (P("gy", "gx"), P("gy", "gx"), P())
    return jax.shard_map(on_device_body, mesh=mesh, in_specs=in_specs, out_specs=out_specs, check_vma=False)
```

```python
import jax
import jax.numpy as jnp
from jax import lax
from jax.experimental import pallas as pl
from jax.experimental.pallas import tpu as pltpu
from jax.sharding import PartitionSpec as P

EPSILON = 1e-06
HALO = 12
LANES = 128


def padded_2(block, sides, width):
    for axis, dim in sides:
        count = lax.axis_size(axis)
        forward = [(i, i + 1) for i in range(count - 1)]
        backward = [(target, source) for source, target in forward]
        low = lax.ppermute(
            lax.slice_in_dim(block, block.shape[dim] - width, None, axis=dim), axis, forward
        )
        high = lax.ppermute(lax.slice_in_dim(block, 0, width, axis=dim), axis, backward)
        block = jnp.concatenate([low, block, high], axis=dim)
    return block


def butterfly_sum(values, axes):
    for axis in axes:
        count = lax.axis_size(axis)
        if count & (count - 1):
            values = lax.psum(values, axis)
            continue
        stride = 1
        while stride < count:
            values = values + lax.ppermute(values, axis, [(i, i ^ stride) for i in range(count)])
            stride *= 2
    return values


SWEEPS = 3
RELAXATION = 0.8
TIME_STEP = 0.1


def make_nb(roll):
    def nb(x, dr, dc):
        if dr:
            x = roll(x, (-dr) % x.shape[0], 0)
        if dc:
            x = roll(x, (-dc) % x.shape[1], 1)
        return x

    return nb


def edges(nb, u, v, h, cov, dr, dc):
    du = nb(u, dr, dc) - u
    dv = nb(v, dr, dc) - v
    s = du * du + dv * dv
    p = jnp.exp(jnp.log(1.0 + s) * (-1.0 / 3.0))
    a = 0.5 * (h + nb(h, dr, dc)) * cov * nb(cov, dr, dc)
    return du, dv, s, p, a, a * p


def sweep_terms(nb, u, v, h, cov, fric, fu, fv):
    de = edges(nb, u, v, h, cov, 0, 1)
    ds = edges(nb, u, v, h, cov, 1, 0)
    ce, cs = de[5], ds[5]
    fe_u, fe_v = ce * de[0], ce * de[1]
    fs_u, fs_v = cs * ds[0], cs * ds[1]
    flux_u = fe_u + fs_u - nb(fe_u, 0, -1) - nb(fs_u, -1, 0)
    flux_v = fe_v + fs_v - nb(fe_v, 0, -1) - nb(fs_v, -1, 0)
    c_sum = ce + cs + nb(ce, 0, -1) + nb(cs, -1, 0)
    r_u = fu - fric * u + flux_u
    r_v = fv - fric * v + flux_v
    d = 1.0 + fric + c_sum
    return de, ds, r_u, r_v, d


def sweep_fwd(nb, u, v, h, cov, fric, fu, fv):
    de, ds, r_u, r_v, d = sweep_terms(nb, u, v, h, cov, fric, fu, fv)
    return cov * (u + RELAXATION * r_u / d), cov * (v + RELAXATION * r_v / d)


def sweep_bwd(nb, u, v, h, cov, fric, su, sv, bu, bv):
    de, ds, r_u, r_v, d = sweep_terms(nb, u, v, h, cov, fric, h * su, h * sv)
    qu, qv = cov * bu, cov * bv
    tu, tv = RELAXATION * qu / d, RELAXATION * qv / d
    d_bar = -(tu * r_u + tv * r_v) / d
    f_bar = d_bar - (tu * u + tv * v)
    h_bar = tu * su + tv * sv
    wu = qu - fric * tu
    wv = qv - fric * tv
    for (du, dv, s, p, a, c), (dr, dc) in ((de, (0, 1)), (ds, (1, 0))):
        big_u = tu - nb(tu, dr, dc)
        big_v = tv - nb(tv, dr, dc)
        c_bar = big_u * du + big_v * dv + d_bar + nb(d_bar, dr, dc)
        a_bar = c_bar * p
        s_bar = c_bar * a * (-1.0 / 3.0) * p / (1.0 + s)
        gu = big_u * c + 2.0 * s_bar * du
        gv = big_v * c + 2.0 * s_bar * dv
        wu = wu - gu + nb(gu, -dr, -dc)
        wv = wv - gv + nb(gv, -dr, -dc)
        k = 0.5 * cov * nb(cov, dr, dc) * a_bar
        h_bar = h_bar + k + nb(k, -dr, -dc)
    return wu, wv, h_bar, f_bar


def transport_bwd(nb, u, v, h, cov, don_e, don_s, g):
    q = cov * g
    h_bar = q
    div_bar = -TIME_STEP * q
    u_bar = None
    v_bar = None
    for vel, don, (dr, dc) in ((u, don_e, (0, 1)), (v, don_s, (1, 0))):
        f_bar = div_bar - nb(div_bar, dr, dc)
        kk = cov * nb(cov, dr, dc)
        speed = 0.5 * (vel + nb(vel, dr, dc))
        hh = don * h + (1.0 - don) * nb(h, dr, dc)
        x = 0.5 * f_bar * kk * hh
        vb = x + nb(x, -dr, -dc)
        y = f_bar * speed * kk
        h_bar = h_bar + y * don + nb(y * (1.0 - don), -dr, -dc)
        if u_bar is None:
            u_bar = vb
        else:
            v_bar = vb
    return u_bar, v_bar, h_bar


def statics(f):
    mask = f["mask"]
    cov = (mask > 0.5).astype(jnp.float32)
    grounded = (mask > 1.5).astype(jnp.float32)
    flags = f["flags"]
    don_s = (flags > 1.5).astype(jnp.float32)
    don_e = flags - 2.0 * don_s
    fric = f["beta"] * grounded
    return cov, grounded, don_e, don_s, fric


def forward_all(nb, f, steps):
    cov, grounded, don_e, don_s, fric = statics(f)
    out = []
    for n in range(steps):
        h = f["thick"][n]
        u, v = f["vel"][n]
        fu, fv = h * f["slope"][0], h * f["slope"][1]
        for _ in range(SWEEPS):
            u, v = sweep_fwd(nb, u, v, h, cov, fric, fu, fv)
        out.append((u, v))
    return out


def backward_all(nb, f, steps, scales, g):
    cov, grounded, don_e, don_s, fric = statics(f)
    su, sv = f["slope"][0], f["slope"][1]
    beta = jnp.zeros_like(g)
    for n in reversed(range(steps)):
        h = f["thick"][n]
        u, v = f["vel"][n]
        fu, fv = h * su, h * sv
        states = []
        for _ in range(SWEEPS):
            states.append((u, v))
            u, v = sweep_fwd(nb, u, v, h, cov, fric, fu, fv)
        ou, ov = f["obs"][n]
        inv = 1.0 / scales[n]
        bu, bv, h_bar = transport_bwd(nb, u, v, h, cov, don_e, don_s, g)
        bu = bu + grounded * (u - ou) * inv
        bv = bv + grounded * (v - ov) * inv
        f_tot = jnp.zeros_like(g)
        for k in reversed(range(SWEEPS)):
            wu, wv = states[k]
            bu, bv, hb, fb = sweep_bwd(nb, wu, wv, h, cov, fric, su, sv, bu, bv)
            h_bar = h_bar + hb
            f_tot = f_tot + fb
        beta = beta + grounded * f_tot
        g = h_bar
    return beta, g


def unpack(arr, steps):
    return {
        "mask": arr[0],
        "flags": arr[1],
        "beta": arr[2],
        "slope": (arr[3], arr[4]),
        "thick": [arr[5 + n] for n in range(steps)],
        "vel": [(arr[5 + steps + 2 * n], arr[6 + steps + 2 * n]) for n in range(steps)],
        "obs": [(arr[5 + 3 * steps + 2 * n], arr[6 + 3 * steps + 2 * n]) for n in range(steps)],
        "adj": arr[5 + 5 * steps],
    }


class RefLoader:
    def __init__(self, ref, steps):
        self.ref = ref
        self.steps = steps

    def __getitem__(self, key):
        r, steps = self.ref, self.steps
        if key == "mask":
            return r[0]
        if key == "flags":
            return r[1]
        if key == "beta":
            return r[2]
        if key == "slope":
            return (r[3], r[4])
        if key == "thick":
            return [r[5 + n] for n in range(steps)]
        if key == "vel":
            return [(r[5 + steps + 2 * n], r[6 + steps + 2 * n]) for n in range(steps)]
        if key == "obs":
            return [(r[5 + 3 * steps + 2 * n], r[6 + 3 * steps + 2 * n]) for n in range(steps)]
        if key == "adj":
            return r[5 + 5 * steps]
        raise KeyError(key)


def forward_kernel(steps):
    def kernel(f_ref, o_ref):
        nb = make_nb(pltpu.roll)
        out = forward_all(nb, RefLoader(f_ref, steps), steps)
        for n, (u, v) in enumerate(out):
            o_ref[2 * n] = u
            o_ref[2 * n + 1] = v

    return kernel


def backward_kernel(steps):
    def kernel(s_ref, f_ref, o_ref):
        nb = make_nb(pltpu.roll)
        loader = RefLoader(f_ref, steps)
        scales = [s_ref[n] for n in range(steps)]
        beta, g = backward_all(nb, loader, steps, scales, loader["adj"])
        o_ref[0] = beta
        o_ref[1] = g

    return kernel


def run_forward(fields, steps):
    _, r, c = fields.shape
    return pl.pallas_call(
        forward_kernel(steps),
        out_shape=jax.ShapeDtypeStruct((2 * steps, r, c), jnp.float32),
        in_specs=[pl.BlockSpec(memory_space=pltpu.VMEM)],
        out_specs=pl.BlockSpec(memory_space=pltpu.VMEM),
    )(fields)


def run_backward(scales, fields, steps):
    _, r, c = fields.shape
    return pl.pallas_call(
        backward_kernel(steps),
        out_shape=jax.ShapeDtypeStruct((2, r, c), jnp.float32),
        in_specs=[pl.BlockSpec(memory_space=pltpu.SMEM), pl.BlockSpec(memory_space=pltpu.VMEM)],
        out_specs=pl.BlockSpec(memory_space=pltpu.VMEM),
    )(scales, fields)


def on_device(
    saved_thickness,
    saved_velocity,
    surface_slope,
    basal_beta,
    cell_mask,
    upwind_flags,
    observed_velocity,
    thickness_adjoint,
):
    steps = saved_thickness.shape[0]
    rows, cols = basal_beta.shape
    f32 = jnp.float32
    obs_local = observed_velocity.astype(f32)
    grounded_local = (cell_mask == 2).astype(f32)
    scale_local = [
        jnp.sum(grounded_local * jnp.sum(obs_local[n] * obs_local[n], axis=0)) for n in range(steps)
    ]
    fields = jnp.concatenate(
        [
            jnp.stack([cell_mask.astype(f32), upwind_flags.astype(f32), basal_beta]),
            surface_slope.astype(f32),
            saved_thickness.astype(f32),
            saved_velocity.astype(f32).reshape(steps * 2, rows, cols),
            obs_local.reshape(steps * 2, rows, cols),
            thickness_adjoint[None],
        ],
        axis=0,
    )
    wide = padded_2(fields, (("gy", 1), ("gx", 2)), HALO)
    wide_cols = -(-wide.shape[2] // LANES) * LANES
    wide = jnp.pad(wide, ((0, 0), (0, 0), (0, wide_cols - wide.shape[2])))

    def centre(values):
        return values[..., HALO : HALO + rows, HALO : HALO + cols]

    velocities = run_forward(wide, steps)
    misfit_local = []
    for n in range(steps):
        difference = centre(velocities[2 * n : 2 * n + 2]) - obs_local[n]
        misfit_local.append(0.5 * jnp.sum(grounded_local * jnp.sum(difference * difference, axis=0)))
    totals = butterfly_sum(jnp.stack(scale_local + misfit_local), ("gx", "gy"))
    cell_count = rows * cols * lax.axis_size("gy") * lax.axis_size("gx")
    scales = totals[:steps] / cell_count + EPSILON
    misfit = jnp.zeros((), f32)
    for n in reversed(range(steps)):
        misfit = misfit + totals[steps + n] / cell_count / scales[n]
    grads = run_backward(scales, wide, steps)
    return (centre(grads[0]), centre(grads[1]), misfit)


def solution(mesh):
    in_specs = (
        P(None, "gy", "gx"),
        P(None, None, "gy", "gx"),
        P(None, "gy", "gx"),
        P("gy", "gx"),
        P("gy", "gx"),
        P("gy", "gx"),
        P(None, None, "gy", "gx"),
        P("gy", "gx"),
    )
    out_specs = (P("gy", "gx"), P("gy", "gx"), P())
    return jax.shard_map(
        on_device, mesh=mesh, in_specs=in_specs, out_specs=out_specs, check_vma=False
    )
```

```python
import jax
import jax.numpy as jnp
from jax import lax
from jax.experimental import pallas as pl
from jax.experimental.pallas import tpu as pltpu
from jax.sharding import PartitionSpec as P

EPSILON = 1e-06
HALO = 12
LANES = 128


def wrapped_patch(block, width):
    pieces = {}
    for axis, dim in (("gy", 1), ("gx", 2)):
        count = lax.axis_size(axis)
        forward = [(i, i + 1) for i in range(count - 1)]
        backward = [(target, source) for source, target in forward]
        before = lax.ppermute(
            lax.slice_in_dim(block, block.shape[dim] - width, None, axis=dim), axis, forward
        )
        after = lax.ppermute(lax.slice_in_dim(block, 0, width, axis=dim), axis, backward)
        if dim == 1:
            block = jnp.concatenate([block, after, before], axis=dim)
        else:
            lanes = -(-(block.shape[2] + 2 * width) // LANES) * LANES
            gap = jnp.zeros(block.shape[:2] + (lanes - block.shape[2] - 2 * width,), block.dtype)
            block = jnp.concatenate([block, after, gap, before], axis=dim)
    return block


def butterfly_sum(values, axes):
    for axis in axes:
        count = lax.axis_size(axis)
        if count & (count - 1):
            values = lax.psum(values, axis)
            continue
        stride = 1
        while stride < count:
            values = values + lax.ppermute(values, axis, [(i, i ^ stride) for i in range(count)])
            stride *= 2
    return values


SWEEPS = 3
RELAXATION = 0.8
TIME_STEP = 0.1


def make_nb(roll):
    def nb(x, dr, dc):
        if dr:
            x = roll(x, (-dr) % x.shape[0], 0)
        if dc:
            x = roll(x, (-dc) % x.shape[1], 1)
        return x

    return nb


def edges(nb, u, v, h, cov, dr, dc):
    du = nb(u, dr, dc) - u
    dv = nb(v, dr, dc) - v
    s = du * du + dv * dv
    p = jnp.exp(jnp.log(1.0 + s) * (-1.0 / 3.0))
    a = 0.5 * (h + nb(h, dr, dc)) * cov * nb(cov, dr, dc)
    return du, dv, s, p, a, a * p


def sweep_terms(nb, u, v, h, cov, fric, fu, fv):
    de = edges(nb, u, v, h, cov, 0, 1)
    ds = edges(nb, u, v, h, cov, 1, 0)
    ce, cs = de[5], ds[5]
    fe_u, fe_v = ce * de[0], ce * de[1]
    fs_u, fs_v = cs * ds[0], cs * ds[1]
    flux_u = fe_u + fs_u - nb(fe_u, 0, -1) - nb(fs_u, -1, 0)
    flux_v = fe_v + fs_v - nb(fe_v, 0, -1) - nb(fs_v, -1, 0)
    c_sum = ce + cs + nb(ce, 0, -1) + nb(cs, -1, 0)
    r_u = fu - fric * u + flux_u
    r_v = fv - fric * v + flux_v
    d = 1.0 + fric + c_sum
    return de, ds, r_u, r_v, d


def sweep_fwd(nb, u, v, h, cov, fric, fu, fv):
    de, ds, r_u, r_v, d = sweep_terms(nb, u, v, h, cov, fric, fu, fv)
    return cov * (u + RELAXATION * r_u / d), cov * (v + RELAXATION * r_v / d)


def sweep_bwd(nb, u, v, h, cov, fric, su, sv, bu, bv):
    de, ds, r_u, r_v, d = sweep_terms(nb, u, v, h, cov, fric, h * su, h * sv)
    qu, qv = cov * bu, cov * bv
    tu, tv = RELAXATION * qu / d, RELAXATION * qv / d
    d_bar = -(tu * r_u + tv * r_v) / d
    f_bar = d_bar - (tu * u + tv * v)
    h_bar = tu * su + tv * sv
    wu = qu - fric * tu
    wv = qv - fric * tv
    for (du, dv, s, p, a, c), (dr, dc) in ((de, (0, 1)), (ds, (1, 0))):
        big_u = tu - nb(tu, dr, dc)
        big_v = tv - nb(tv, dr, dc)
        c_bar = big_u * du + big_v * dv + d_bar + nb(d_bar, dr, dc)
        a_bar = c_bar * p
        s_bar = c_bar * a * (-1.0 / 3.0) * p / (1.0 + s)
        gu = big_u * c + 2.0 * s_bar * du
        gv = big_v * c + 2.0 * s_bar * dv
        wu = wu - gu + nb(gu, -dr, -dc)
        wv = wv - gv + nb(gv, -dr, -dc)
        k = 0.5 * cov * nb(cov, dr, dc) * a_bar
        h_bar = h_bar + k + nb(k, -dr, -dc)
    return wu, wv, h_bar, f_bar


def transport_bwd(nb, u, v, h, cov, don_e, don_s, g):
    q = cov * g
    h_bar = q
    div_bar = -TIME_STEP * q
    u_bar = None
    v_bar = None
    for vel, don, (dr, dc) in ((u, don_e, (0, 1)), (v, don_s, (1, 0))):
        f_bar = div_bar - nb(div_bar, dr, dc)
        kk = cov * nb(cov, dr, dc)
        speed = 0.5 * (vel + nb(vel, dr, dc))
        hh = don * h + (1.0 - don) * nb(h, dr, dc)
        x = 0.5 * f_bar * kk * hh
        vb = x + nb(x, -dr, -dc)
        y = f_bar * speed * kk
        h_bar = h_bar + y * don + nb(y * (1.0 - don), -dr, -dc)
        if u_bar is None:
            u_bar = vb
        else:
            v_bar = vb
    return u_bar, v_bar, h_bar


def statics(f):
    mask = f["mask"]
    cov = (mask > 0.5).astype(jnp.float32)
    grounded = (mask > 1.5).astype(jnp.float32)
    flags = f["flags"]
    don_s = (flags > 1.5).astype(jnp.float32)
    don_e = flags - 2.0 * don_s
    fric = f["beta"] * grounded
    return cov, grounded, don_e, don_s, fric


def forward_all(nb, f, steps):
    cov, grounded, don_e, don_s, fric = statics(f)
    out = []
    for n in range(steps):
        h = f["thick"][n]
        u, v = f["vel"][n]
        fu, fv = h * f["slope"][0], h * f["slope"][1]
        for _ in range(SWEEPS):
            u, v = sweep_fwd(nb, u, v, h, cov, fric, fu, fv)
        out.append((u, v))
    return out


def backward_all(nb, f, steps, scales, g):
    cov, grounded, don_e, don_s, fric = statics(f)
    su, sv = f["slope"][0], f["slope"][1]
    beta = jnp.zeros_like(g)
    for n in reversed(range(steps)):
        h = f["thick"][n]
        u, v = f["vel"][n]
        fu, fv = h * su, h * sv
        states = []
        for _ in range(SWEEPS):
            states.append((u, v))
            u, v = sweep_fwd(nb, u, v, h, cov, fric, fu, fv)
        ou, ov = f["obs"][n]
        inv = 1.0 / scales[n]
        bu, bv, h_bar = transport_bwd(nb, u, v, h, cov, don_e, don_s, g)
        bu = bu + grounded * (u - ou) * inv
        bv = bv + grounded * (v - ov) * inv
        f_tot = jnp.zeros_like(g)
        for k in reversed(range(SWEEPS)):
            wu, wv = states[k]
            bu, bv, hb, fb = sweep_bwd(nb, wu, wv, h, cov, fric, su, sv, bu, bv)
            h_bar = h_bar + hb
            f_tot = f_tot + fb
        beta = beta + grounded * f_tot
        g = h_bar
    return beta, g


def unpack(arr, steps):
    return {
        "mask": arr[0],
        "flags": arr[1],
        "beta": arr[2],
        "slope": (arr[3], arr[4]),
        "thick": [arr[5 + n] for n in range(steps)],
        "vel": [(arr[5 + steps + 2 * n], arr[6 + steps + 2 * n]) for n in range(steps)],
        "obs": [(arr[5 + 3 * steps + 2 * n], arr[6 + 3 * steps + 2 * n]) for n in range(steps)],
        "adj": arr[5 + 5 * steps],
    }


class RefLoader:
    def __init__(self, ref, steps):
        self.ref = ref
        self.steps = steps

    def __getitem__(self, key):
        r, steps = self.ref, self.steps
        if key == "mask":
            return r[0]
        if key == "flags":
            return r[1]
        if key == "beta":
            return r[2]
        if key == "slope":
            return (r[3], r[4])
        if key == "thick":
            return [r[5 + n] for n in range(steps)]
        if key == "vel":
            return [(r[5 + steps + 2 * n], r[6 + steps + 2 * n]) for n in range(steps)]
        if key == "obs":
            return [(r[5 + 3 * steps + 2 * n], r[6 + 3 * steps + 2 * n]) for n in range(steps)]
        if key == "adj":
            return r[5 + 5 * steps]
        raise KeyError(key)


def forward_kernel(steps, rows, cols):
    def kernel(f_ref, o_ref):
        nb = make_nb(pltpu.roll)
        loader = RefLoader(f_ref, steps)
        out = forward_all(nb, loader, steps)
        grounded = (loader["mask"][:rows, :cols] > 1.5).astype(jnp.float32)

        def total(x):
            return jnp.broadcast_to(jnp.sum(jnp.sum(x, axis=0, keepdims=True), axis=1, keepdims=True), o_ref.shape[1:])

        for n, (u, v) in enumerate(out):
            ou, ov = loader["obs"][n]
            ou, ov = ou[:rows, :cols], ov[:rows, :cols]
            du, dv = u[:rows, :cols] - ou, v[:rows, :cols] - ov
            o_ref[n] = total(grounded * (ou * ou + ov * ov))
            o_ref[steps + n] = total(0.5 * grounded * (du * du + dv * dv))

    return kernel


def backward_kernel(steps, rows, cols):
    def kernel(s_ref, f_ref, o_ref):
        nb = make_nb(pltpu.roll)
        loader = RefLoader(f_ref, steps)
        scales = [s_ref[n] for n in range(steps)]
        beta, g = backward_all(nb, loader, steps, scales, loader["adj"])
        o_ref[0] = beta[: o_ref.shape[1], : o_ref.shape[2]]
        o_ref[1] = g[: o_ref.shape[1], : o_ref.shape[2]]

    return kernel


def run_forward(fields, steps, rows, cols):
    return pl.pallas_call(
        forward_kernel(steps, rows, cols),
        out_shape=jax.ShapeDtypeStruct((2 * steps, 8, LANES), jnp.float32),
        in_specs=[pl.BlockSpec(memory_space=pltpu.VMEM)],
        out_specs=pl.BlockSpec(memory_space=pltpu.VMEM),
    )(fields)


def run_backward(scales, fields, steps, rows, cols):
    return pl.pallas_call(
        backward_kernel(steps, rows, cols),
        out_shape=jax.ShapeDtypeStruct((2, rows, cols), jnp.float32),
        in_specs=[pl.BlockSpec(memory_space=pltpu.SMEM), pl.BlockSpec(memory_space=pltpu.VMEM)],
        out_specs=pl.BlockSpec(memory_space=pltpu.VMEM),
    )(scales, fields)


def on_device(
    saved_thickness,
    saved_velocity,
    surface_slope,
    basal_beta,
    cell_mask,
    upwind_flags,
    observed_velocity,
    thickness_adjoint,
):
    steps = saved_thickness.shape[0]
    rows, cols = basal_beta.shape
    f32 = jnp.float32
    fields = jnp.concatenate(
        [
            jnp.stack([cell_mask.astype(f32), upwind_flags.astype(f32), basal_beta]),
            surface_slope.astype(f32),
            saved_thickness.astype(f32),
            saved_velocity.astype(f32).reshape(steps * 2, rows, cols),
            observed_velocity.astype(f32).reshape(steps * 2, rows, cols),
            thickness_adjoint[None],
        ],
        axis=0,
    )
    wide = wrapped_patch(fields, HALO)
    local_sums = run_forward(wide, steps, rows, cols)[:, 0, 0]
    totals = butterfly_sum(local_sums, ("gx", "gy"))
    cell_count = rows * cols * lax.axis_size("gy") * lax.axis_size("gx")
    scales = totals[:steps] / cell_count + EPSILON
    misfit = jnp.zeros((), f32)
    for n in reversed(range(steps)):
        misfit = misfit + totals[steps + n] / cell_count / scales[n]
    grads = run_backward(scales, wide, steps, rows, cols)
    return (grads[0], grads[1], misfit)


def solution(mesh):
    in_specs = (
        P(None, "gy", "gx"),
        P(None, None, "gy", "gx"),
        P(None, "gy", "gx"),
        P("gy", "gx"),
        P("gy", "gx"),
        P("gy", "gx"),
        P(None, None, "gy", "gx"),
        P("gy", "gx"),
    )
    out_specs = (P("gy", "gx"), P("gy", "gx"), P())
    return jax.shard_map(
        on_device, mesh=mesh, in_specs=in_specs, out_specs=out_specs, check_vma=False
    )
```

```python
import jax
import jax.numpy as jnp
from jax import lax
from jax.experimental import pallas as pl
from jax.experimental.pallas import tpu as pltpu
from jax.sharding import PartitionSpec as P

EPSILON = 1e-06
HALO = 12
LANES = 128


def wrapped_patch(block, width):
    pieces = {}
    for axis, dim in (("gy", 1), ("gx", 2)):
        count = lax.axis_size(axis)
        forward = [(i, i + 1) for i in range(count - 1)]
        backward = [(target, source) for source, target in forward]
        before = lax.ppermute(
            lax.slice_in_dim(block, block.shape[dim] - width, None, axis=dim), axis, forward
        )
        after = lax.ppermute(lax.slice_in_dim(block, 0, width, axis=dim), axis, backward)
        if dim == 1:
            block = jnp.concatenate([block, after, before], axis=dim)
        else:
            lanes = -(-(block.shape[2] + 2 * width) // LANES) * LANES
            gap = jnp.zeros(block.shape[:2] + (lanes - block.shape[2] - 2 * width,), block.dtype)
            block = jnp.concatenate([block, after, gap, before], axis=dim)
    return block


def butterfly_sum(values, axes):
    for axis in axes:
        count = lax.axis_size(axis)
        if count & (count - 1):
            values = lax.psum(values, axis)
            continue
        stride = 1
        while stride < count:
            values = values + lax.ppermute(values, axis, [(i, i ^ stride) for i in range(count)])
            stride *= 2
    return values


SWEEPS = 3
RELAXATION = 0.8
TIME_STEP = 0.1


def make_nb(roll):
    def nb(x, dr, dc):
        if dr:
            x = roll(x, (-dr) % x.shape[0], 0)
        if dc:
            x = roll(x, (-dc) % x.shape[1], 1)
        return x

    return nb


def edges(nb, u, v, h, cov, dr, dc):
    du = nb(u, dr, dc) - u
    dv = nb(v, dr, dc) - v
    s = du * du + dv * dv
    p = jnp.exp(jnp.log(1.0 + s) * (-1.0 / 3.0))
    a = 0.5 * (h + nb(h, dr, dc)) * cov * nb(cov, dr, dc)
    return du, dv, s, p, a, a * p


def sweep_terms(nb, u, v, h, cov, fric, fu, fv):
    de = edges(nb, u, v, h, cov, 0, 1)
    ds = edges(nb, u, v, h, cov, 1, 0)
    ce, cs = de[5], ds[5]
    fe_u, fe_v = ce * de[0], ce * de[1]
    fs_u, fs_v = cs * ds[0], cs * ds[1]
    flux_u = fe_u + fs_u - nb(fe_u, 0, -1) - nb(fs_u, -1, 0)
    flux_v = fe_v + fs_v - nb(fe_v, 0, -1) - nb(fs_v, -1, 0)
    c_sum = ce + cs + nb(ce, 0, -1) + nb(cs, -1, 0)
    r_u = fu - fric * u + flux_u
    r_v = fv - fric * v + flux_v
    d = 1.0 + fric + c_sum
    return de, ds, r_u, r_v, d


def sweep_fwd(nb, u, v, h, cov, fric, fu, fv):
    de, ds, r_u, r_v, d = sweep_terms(nb, u, v, h, cov, fric, fu, fv)
    return cov * (u + RELAXATION * r_u / d), cov * (v + RELAXATION * r_v / d)


def sweep_bwd(nb, u, v, h, cov, fric, su, sv, bu, bv):
    de, ds, r_u, r_v, d = sweep_terms(nb, u, v, h, cov, fric, h * su, h * sv)
    qu, qv = cov * bu, cov * bv
    tu, tv = RELAXATION * qu / d, RELAXATION * qv / d
    d_bar = -(tu * r_u + tv * r_v) / d
    f_bar = d_bar - (tu * u + tv * v)
    h_bar = tu * su + tv * sv
    wu = qu - fric * tu
    wv = qv - fric * tv
    for (du, dv, s, p, a, c), (dr, dc) in ((de, (0, 1)), (ds, (1, 0))):
        big_u = tu - nb(tu, dr, dc)
        big_v = tv - nb(tv, dr, dc)
        c_bar = big_u * du + big_v * dv + d_bar + nb(d_bar, dr, dc)
        a_bar = c_bar * p
        s_bar = c_bar * a * (-1.0 / 3.0) * p / (1.0 + s)
        gu = big_u * c + 2.0 * s_bar * du
        gv = big_v * c + 2.0 * s_bar * dv
        wu = wu - gu + nb(gu, -dr, -dc)
        wv = wv - gv + nb(gv, -dr, -dc)
        k = 0.5 * cov * nb(cov, dr, dc) * a_bar
        h_bar = h_bar + k + nb(k, -dr, -dc)
    return wu, wv, h_bar, f_bar


def transport_bwd(nb, u, v, h, cov, don_e, don_s, g):
    q = cov * g
    h_bar = q
    div_bar = -TIME_STEP * q
    u_bar = None
    v_bar = None
    for vel, don, (dr, dc) in ((u, don_e, (0, 1)), (v, don_s, (1, 0))):
        f_bar = div_bar - nb(div_bar, dr, dc)
        kk = cov * nb(cov, dr, dc)
        speed = 0.5 * (vel + nb(vel, dr, dc))
        hh = don * h + (1.0 - don) * nb(h, dr, dc)
        x = 0.5 * f_bar * kk * hh
        vb = x + nb(x, -dr, -dc)
        y = f_bar * speed * kk
        h_bar = h_bar + y * don + nb(y * (1.0 - don), -dr, -dc)
        if u_bar is None:
            u_bar = vb
        else:
            v_bar = vb
    return u_bar, v_bar, h_bar


def statics(f):
    mask = f["mask"]
    cov = (mask > 0.5).astype(jnp.float32)
    grounded = (mask > 1.5).astype(jnp.float32)
    flags = f["flags"]
    don_s = (flags > 1.5).astype(jnp.float32)
    don_e = flags - 2.0 * don_s
    fric = f["beta"] * grounded
    return cov, grounded, don_e, don_s, fric


def forward_all(nb, f, steps):
    cov, grounded, don_e, don_s, fric = statics(f)
    out = []
    for n in range(steps):
        h = f["thick"][n]
        u, v = f["vel"][n]
        fu, fv = h * f["slope"][0], h * f["slope"][1]
        for _ in range(SWEEPS):
            u, v = sweep_fwd(nb, u, v, h, cov, fric, fu, fv)
        out.append((u, v))
    return out


def backward_all(nb, f, steps, scales, g):
    cov, grounded, don_e, don_s, fric = statics(f)
    su, sv = f["slope"][0], f["slope"][1]
    beta = jnp.zeros_like(g)
    for n in reversed(range(steps)):
        h = f["thick"][n]
        u, v = f["vel"][n]
        fu, fv = h * su, h * sv
        states = []
        for _ in range(SWEEPS):
            states.append((u, v))
            u, v = sweep_fwd(nb, u, v, h, cov, fric, fu, fv)
        ou, ov = f["obs"][n]
        inv = 1.0 / scales[n]
        bu, bv, h_bar = transport_bwd(nb, u, v, h, cov, don_e, don_s, g)
        bu = bu + grounded * (u - ou) * inv
        bv = bv + grounded * (v - ov) * inv
        f_tot = jnp.zeros_like(g)
        for k in reversed(range(SWEEPS)):
            wu, wv = states[k]
            bu, bv, hb, fb = sweep_bwd(nb, wu, wv, h, cov, fric, su, sv, bu, bv)
            h_bar = h_bar + hb
            f_tot = f_tot + fb
        beta = beta + grounded * f_tot
        g = h_bar
    return beta, g


def unpack(arr, steps):
    return {
        "mask": arr[0],
        "flags": arr[1],
        "beta": arr[2],
        "slope": (arr[3], arr[4]),
        "thick": [arr[5 + n] for n in range(steps)],
        "vel": [(arr[5 + steps + 2 * n], arr[6 + steps + 2 * n]) for n in range(steps)],
        "obs": [(arr[5 + 3 * steps + 2 * n], arr[6 + 3 * steps + 2 * n]) for n in range(steps)],
        "adj": arr[5 + 5 * steps],
    }


class RefLoader:
    def __init__(self, ref, steps):
        self.ref = ref
        self.steps = steps

    def __getitem__(self, key):
        r, steps = self.ref, self.steps
        if key == "mask":
            return r[0]
        if key == "flags":
            return r[1]
        if key == "beta":
            return r[2]
        if key == "slope":
            return (r[3], r[4])
        if key == "thick":
            return [r[5 + n] for n in range(steps)]
        if key == "vel":
            return [(r[5 + steps + 2 * n], r[6 + steps + 2 * n]) for n in range(steps)]
        if key == "obs":
            return [(r[5 + 3 * steps + 2 * n], r[6 + 3 * steps + 2 * n]) for n in range(steps)]
        if key == "adj":
            return r[5 + 5 * steps]
        raise KeyError(key)


def forward_kernel(steps, rows, cols):
    def kernel(f_ref, o_ref):
        nb = make_nb(pltpu.roll)
        loader = RefLoader(f_ref, steps)
        out = forward_all(nb, loader, steps)
        grounded = (loader["mask"][:rows, :cols] > 1.5).astype(jnp.float32)

        def total(x):
            return jnp.broadcast_to(jnp.sum(jnp.sum(x, axis=0, keepdims=True), axis=1, keepdims=True), o_ref.shape[1:])

        for n, (u, v) in enumerate(out):
            ou, ov = loader["obs"][n]
            ou, ov = ou[:rows, :cols], ov[:rows, :cols]
            du, dv = u[:rows, :cols] - ou, v[:rows, :cols] - ov
            o_ref[n] = total(grounded * (ou * ou + ov * ov))
            o_ref[steps + n] = total(0.5 * grounded * (du * du + dv * dv))

    return kernel


def backward_kernel(steps, rows, cols):
    def kernel(s_ref, f_ref, beta_ref, g_ref):
        nb = make_nb(pltpu.roll)
        loader = RefLoader(f_ref, steps)
        scales = [s_ref[n] for n in range(steps)]
        beta, g = backward_all(nb, loader, steps, scales, loader["adj"])
        beta_ref[...] = beta[:rows, :cols]
        g_ref[...] = g[:rows, :cols]

    return kernel


def pack_kernel(steps):
    def kernel(thick_ref, vel_ref, slope_ref, beta_ref, mask_ref, flags_ref, obs_ref, adj_ref, o_ref):
        f32 = jnp.float32
        o_ref[0] = mask_ref[...].astype(f32)
        o_ref[1] = flags_ref[...].astype(f32)
        o_ref[2] = beta_ref[...]
        for c in range(2):
            o_ref[3 + c] = slope_ref[c].astype(f32)
        for n in range(steps):
            o_ref[5 + n] = thick_ref[n].astype(f32)
            for c in range(2):
                o_ref[5 + steps + 2 * n + c] = vel_ref[n, c].astype(f32)
                o_ref[5 + 3 * steps + 2 * n + c] = obs_ref[n, c].astype(f32)
        o_ref[5 + 5 * steps] = adj_ref[...]

    return kernel


def run_pack(*arrays):
    steps, rows, cols = arrays[0].shape
    return pl.pallas_call(
        pack_kernel(steps),
        out_shape=jax.ShapeDtypeStruct((6 + 5 * steps, rows, cols), jnp.float32),
        in_specs=[pl.BlockSpec(memory_space=pltpu.VMEM)] * len(arrays),
        out_specs=pl.BlockSpec(memory_space=pltpu.VMEM),
    )(*arrays)


def run_forward(fields, steps, rows, cols):
    return pl.pallas_call(
        forward_kernel(steps, rows, cols),
        out_shape=jax.ShapeDtypeStruct((2 * steps, 8, LANES), jnp.float32),
        in_specs=[pl.BlockSpec(memory_space=pltpu.VMEM)],
        out_specs=pl.BlockSpec(memory_space=pltpu.VMEM),
    )(fields)


def run_backward(scales, fields, steps, rows, cols):
    return pl.pallas_call(
        backward_kernel(steps, rows, cols),
        out_shape=(jax.ShapeDtypeStruct((rows, cols), jnp.float32),) * 2,
        in_specs=[pl.BlockSpec(memory_space=pltpu.SMEM), pl.BlockSpec(memory_space=pltpu.VMEM)],
        out_specs=(pl.BlockSpec(memory_space=pltpu.VMEM),) * 2,
    )(scales, fields)


def on_device(
    saved_thickness,
    saved_velocity,
    surface_slope,
    basal_beta,
    cell_mask,
    upwind_flags,
    observed_velocity,
    thickness_adjoint,
):
    steps = saved_thickness.shape[0]
    rows, cols = basal_beta.shape
    f32 = jnp.float32
    fields = run_pack(
        saved_thickness,
        saved_velocity,
        surface_slope,
        basal_beta,
        cell_mask,
        upwind_flags,
        observed_velocity,
        thickness_adjoint,
    )
    wide = wrapped_patch(fields, HALO)
    local_sums = run_forward(wide, steps, rows, cols)[:, 0, 0]
    totals = butterfly_sum(local_sums, ("gx", "gy"))
    cell_count = rows * cols * lax.axis_size("gy") * lax.axis_size("gx")
    scales = totals[:steps] / cell_count + EPSILON
    misfit = jnp.zeros((), f32)
    for n in reversed(range(steps)):
        misfit = misfit + totals[steps + n] / cell_count / scales[n]
    grads = run_backward(scales, wide, steps, rows, cols)
    return (grads[0], grads[1], misfit)


def solution(mesh):
    in_specs = (
        P(None, "gy", "gx"),
        P(None, None, "gy", "gx"),
        P(None, "gy", "gx"),
        P("gy", "gx"),
        P("gy", "gx"),
        P("gy", "gx"),
        P(None, None, "gy", "gx"),
        P("gy", "gx"),
    )
    out_specs = (P("gy", "gx"), P("gy", "gx"), P())
    return jax.shard_map(
        on_device, mesh=mesh, in_specs=in_specs, out_specs=out_specs, check_vma=False
    )
```

```python
import jax
import jax.numpy as jnp
from jax import lax
from jax.experimental import pallas as pl
from jax.experimental.pallas import tpu as pltpu
from jax.sharding import PartitionSpec as P

EPSILON = 1e-06
HALO = 12
LANES = 128


def wrapped_patch(block, width):
    ny, nx = lax.axis_size("gy"), lax.axis_size("gx")
    rows, cols = block.shape[1], block.shape[2]
    first, last = slice(0, width), slice(rows - width, rows)
    first_c, last_c = slice(0, width), slice(cols - width, cols)
    whole_r, whole_c = slice(0, rows), slice(0, cols)

    def take(dy, dx, row_part, col_part):
        pairs = []
        for iy in range(ny):
            for ix in range(nx):
                ty, tx = iy + dy, ix + dx
                if 0 <= ty < ny and 0 <= tx < nx:
                    pairs.append((iy * nx + ix, ty * nx + tx))
        return lax.ppermute(block[:, row_part, col_part], ("gy", "gx"), pairs)

    north = take(1, 0, last, whole_c)
    south = take(-1, 0, first, whole_c)
    west = take(0, 1, whole_r, last_c)
    east = take(0, -1, whole_r, first_c)
    north_west = take(1, 1, last, last_c)
    north_east = take(1, -1, last, first_c)
    south_west = take(-1, 1, first, last_c)
    south_east = take(-1, -1, first, first_c)
    lanes = -(-(cols + 2 * width) // LANES) * LANES
    gap_width = lanes - cols - 2 * width

    def band(main, after, before):
        gap = jnp.zeros(main.shape[:2] + (gap_width,), main.dtype)
        return jnp.concatenate([main, after, gap, before], axis=2)

    return jnp.concatenate(
        [band(block, east, west), band(south, south_east, south_west), band(north, north_east, north_west)],
        axis=1,
    )


def butterfly_sum(values, axes):
    for axis in axes:
        count = lax.axis_size(axis)
        if count & (count - 1):
            values = lax.psum(values, axis)
            continue
        stride = 1
        while stride < count:
            values = values + lax.ppermute(values, axis, [(i, i ^ stride) for i in range(count)])
            stride *= 2
    return values


SWEEPS = 3
RELAXATION = 0.8
TIME_STEP = 0.1


def make_nb(roll):
    def nb(x, dr, dc):
        if dr:
            x = roll(x, (-dr) % x.shape[0], 0)
        if dc:
            x = roll(x, (-dc) % x.shape[1], 1)
        return x

    return nb


def edges(nb, u, v, h, cov, dr, dc):
    du = nb(u, dr, dc) - u
    dv = nb(v, dr, dc) - v
    s = du * du + dv * dv
    p = jnp.exp(jnp.log(1.0 + s) * (-1.0 / 3.0))
    a = 0.5 * (h + nb(h, dr, dc)) * cov * nb(cov, dr, dc)
    return du, dv, s, p, a, a * p


def sweep_terms(nb, u, v, h, cov, fric, fu, fv):
    de = edges(nb, u, v, h, cov, 0, 1)
    ds = edges(nb, u, v, h, cov, 1, 0)
    ce, cs = de[5], ds[5]
    fe_u, fe_v = ce * de[0], ce * de[1]
    fs_u, fs_v = cs * ds[0], cs * ds[1]
    flux_u = fe_u + fs_u - nb(fe_u, 0, -1) - nb(fs_u, -1, 0)
    flux_v = fe_v + fs_v - nb(fe_v, 0, -1) - nb(fs_v, -1, 0)
    c_sum = ce + cs + nb(ce, 0, -1) + nb(cs, -1, 0)
    r_u = fu - fric * u + flux_u
    r_v = fv - fric * v + flux_v
    d = 1.0 + fric + c_sum
    return de, ds, r_u, r_v, d


def sweep_fwd(nb, u, v, h, cov, fric, fu, fv):
    de, ds, r_u, r_v, d = sweep_terms(nb, u, v, h, cov, fric, fu, fv)
    return cov * (u + RELAXATION * r_u / d), cov * (v + RELAXATION * r_v / d)


def sweep_bwd(nb, u, v, h, cov, fric, su, sv, bu, bv):
    de, ds, r_u, r_v, d = sweep_terms(nb, u, v, h, cov, fric, h * su, h * sv)
    qu, qv = cov * bu, cov * bv
    tu, tv = RELAXATION * qu / d, RELAXATION * qv / d
    d_bar = -(tu * r_u + tv * r_v) / d
    f_bar = d_bar - (tu * u + tv * v)
    h_bar = tu * su + tv * sv
    wu = qu - fric * tu
    wv = qv - fric * tv
    for (du, dv, s, p, a, c), (dr, dc) in ((de, (0, 1)), (ds, (1, 0))):
        big_u = tu - nb(tu, dr, dc)
        big_v = tv - nb(tv, dr, dc)
        c_bar = big_u * du + big_v * dv + d_bar + nb(d_bar, dr, dc)
        a_bar = c_bar * p
        s_bar = c_bar * a * (-1.0 / 3.0) * p / (1.0 + s)
        gu = big_u * c + 2.0 * s_bar * du
        gv = big_v * c + 2.0 * s_bar * dv
        wu = wu - gu + nb(gu, -dr, -dc)
        wv = wv - gv + nb(gv, -dr, -dc)
        k = 0.5 * cov * nb(cov, dr, dc) * a_bar
        h_bar = h_bar + k + nb(k, -dr, -dc)
    return wu, wv, h_bar, f_bar


def transport_bwd(nb, u, v, h, cov, don_e, don_s, g):
    q = cov * g
    h_bar = q
    div_bar = -TIME_STEP * q
    u_bar = None
    v_bar = None
    for vel, don, (dr, dc) in ((u, don_e, (0, 1)), (v, don_s, (1, 0))):
        f_bar = div_bar - nb(div_bar, dr, dc)
        kk = cov * nb(cov, dr, dc)
        speed = 0.5 * (vel + nb(vel, dr, dc))
        hh = don * h + (1.0 - don) * nb(h, dr, dc)
        x = 0.5 * f_bar * kk * hh
        vb = x + nb(x, -dr, -dc)
        y = f_bar * speed * kk
        h_bar = h_bar + y * don + nb(y * (1.0 - don), -dr, -dc)
        if u_bar is None:
            u_bar = vb
        else:
            v_bar = vb
    return u_bar, v_bar, h_bar


def statics(f):
    mask = f["mask"]
    cov = (mask > 0.5).astype(jnp.float32)
    grounded = (mask > 1.5).astype(jnp.float32)
    flags = f["flags"]
    don_s = (flags > 1.5).astype(jnp.float32)
    don_e = flags - 2.0 * don_s
    fric = f["beta"] * grounded
    return cov, grounded, don_e, don_s, fric


def forward_all(nb, f, steps):
    cov, grounded, don_e, don_s, fric = statics(f)
    out = []
    for n in range(steps):
        h = f["thick"][n]
        u, v = f["vel"][n]
        fu, fv = h * f["slope"][0], h * f["slope"][1]
        for _ in range(SWEEPS):
            u, v = sweep_fwd(nb, u, v, h, cov, fric, fu, fv)
        out.append((u, v))
    return out


def backward_all(nb, f, steps, scales, g):
    cov, grounded, don_e, don_s, fric = statics(f)
    su, sv = f["slope"][0], f["slope"][1]
    beta = jnp.zeros_like(g)
    for n in reversed(range(steps)):
        h = f["thick"][n]
        u, v = f["vel"][n]
        fu, fv = h * su, h * sv
        states = []
        for _ in range(SWEEPS):
            states.append((u, v))
            u, v = sweep_fwd(nb, u, v, h, cov, fric, fu, fv)
        ou, ov = f["obs"][n]
        inv = 1.0 / scales[n]
        bu, bv, h_bar = transport_bwd(nb, u, v, h, cov, don_e, don_s, g)
        bu = bu + grounded * (u - ou) * inv
        bv = bv + grounded * (v - ov) * inv
        f_tot = jnp.zeros_like(g)
        for k in reversed(range(SWEEPS)):
            wu, wv = states[k]
            bu, bv, hb, fb = sweep_bwd(nb, wu, wv, h, cov, fric, su, sv, bu, bv)
            h_bar = h_bar + hb
            f_tot = f_tot + fb
        beta = beta + grounded * f_tot
        g = h_bar
    return beta, g


def unpack(arr, steps):
    return {
        "mask": arr[0],
        "flags": arr[1],
        "beta": arr[2],
        "slope": (arr[3], arr[4]),
        "thick": [arr[5 + n] for n in range(steps)],
        "vel": [(arr[5 + steps + 2 * n], arr[6 + steps + 2 * n]) for n in range(steps)],
        "obs": [(arr[5 + 3 * steps + 2 * n], arr[6 + 3 * steps + 2 * n]) for n in range(steps)],
        "adj": arr[5 + 5 * steps],
    }


class RefLoader:
    def __init__(self, ref, steps):
        self.ref = ref
        self.steps = steps

    def __getitem__(self, key):
        r, steps = self.ref, self.steps
        if key == "mask":
            return r[0]
        if key == "flags":
            return r[1]
        if key == "beta":
            return r[2]
        if key == "slope":
            return (r[3], r[4])
        if key == "thick":
            return [r[5 + n] for n in range(steps)]
        if key == "vel":
            return [(r[5 + steps + 2 * n], r[6 + steps + 2 * n]) for n in range(steps)]
        if key == "obs":
            return [(r[5 + 3 * steps + 2 * n], r[6 + 3 * steps + 2 * n]) for n in range(steps)]
        if key == "adj":
            return r[5 + 5 * steps]
        raise KeyError(key)


def forward_kernel(steps, rows, cols):
    def kernel(f_ref, o_ref):
        nb = make_nb(pltpu.roll)
        loader = RefLoader(f_ref, steps)
        out = forward_all(nb, loader, steps)
        grounded = (loader["mask"][:rows, :cols] > 1.5).astype(jnp.float32)

        def total(x):
            return jnp.broadcast_to(jnp.sum(jnp.sum(x, axis=0, keepdims=True), axis=1, keepdims=True), o_ref.shape[1:])

        for n, (u, v) in enumerate(out):
            ou, ov = loader["obs"][n]
            ou, ov = ou[:rows, :cols], ov[:rows, :cols]
            du, dv = u[:rows, :cols] - ou, v[:rows, :cols] - ov
            o_ref[n] = total(grounded * (ou * ou + ov * ov))
            o_ref[steps + n] = total(0.5 * grounded * (du * du + dv * dv))

    return kernel


def backward_kernel(steps, rows, cols):
    def kernel(s_ref, f_ref, beta_ref, g_ref):
        nb = make_nb(pltpu.roll)
        loader = RefLoader(f_ref, steps)
        scales = [s_ref[n] for n in range(steps)]
        beta, g = backward_all(nb, loader, steps, scales, loader["adj"])
        beta_ref[...] = beta[:rows, :cols]
        g_ref[...] = g[:rows, :cols]

    return kernel


def pack_kernel(steps):
    def kernel(thick_ref, vel_ref, slope_ref, beta_ref, mask_ref, flags_ref, obs_ref, adj_ref, o_ref):
        f32 = jnp.float32
        o_ref[0] = mask_ref[...].astype(f32)
        o_ref[1] = flags_ref[...].astype(f32)
        o_ref[2] = beta_ref[...]
        for c in range(2):
            o_ref[3 + c] = slope_ref[c].astype(f32)
        for n in range(steps):
            o_ref[5 + n] = thick_ref[n].astype(f32)
            for c in range(2):
                o_ref[5 + steps + 2 * n + c] = vel_ref[n, c].astype(f32)
                o_ref[5 + 3 * steps + 2 * n + c] = obs_ref[n, c].astype(f32)
        o_ref[5 + 5 * steps] = adj_ref[...]

    return kernel


def run_pack(*arrays):
    steps, rows, cols = arrays[0].shape
    return pl.pallas_call(
        pack_kernel(steps),
        out_shape=jax.ShapeDtypeStruct((6 + 5 * steps, rows, cols), jnp.float32),
        in_specs=[pl.BlockSpec(memory_space=pltpu.VMEM)] * len(arrays),
        out_specs=pl.BlockSpec(memory_space=pltpu.VMEM),
    )(*arrays)


def run_forward(fields, steps, rows, cols):
    return pl.pallas_call(
        forward_kernel(steps, rows, cols),
        out_shape=jax.ShapeDtypeStruct((2 * steps, 8, LANES), jnp.float32),
        in_specs=[pl.BlockSpec(memory_space=pltpu.VMEM)],
        out_specs=pl.BlockSpec(memory_space=pltpu.VMEM),
    )(fields)


def run_backward(scales, fields, steps, rows, cols):
    return pl.pallas_call(
        backward_kernel(steps, rows, cols),
        out_shape=(jax.ShapeDtypeStruct((rows, cols), jnp.float32),) * 2,
        in_specs=[pl.BlockSpec(memory_space=pltpu.SMEM), pl.BlockSpec(memory_space=pltpu.VMEM)],
        out_specs=(pl.BlockSpec(memory_space=pltpu.VMEM),) * 2,
    )(scales, fields)


def on_device(
    saved_thickness,
    saved_velocity,
    surface_slope,
    basal_beta,
    cell_mask,
    upwind_flags,
    observed_velocity,
    thickness_adjoint,
):
    steps = saved_thickness.shape[0]
    rows, cols = basal_beta.shape
    f32 = jnp.float32
    fields = run_pack(
        saved_thickness,
        saved_velocity,
        surface_slope,
        basal_beta,
        cell_mask,
        upwind_flags,
        observed_velocity,
        thickness_adjoint,
    )
    wide = wrapped_patch(fields, HALO)
    local_sums = run_forward(wide, steps, rows, cols)[:, 0, 0]
    totals = butterfly_sum(local_sums, ("gx", "gy"))
    cell_count = rows * cols * lax.axis_size("gy") * lax.axis_size("gx")
    scales = totals[:steps] / cell_count + EPSILON
    misfit = jnp.zeros((), f32)
    for n in reversed(range(steps)):
        misfit = misfit + totals[steps + n] / cell_count / scales[n]
    grads = run_backward(scales, wide, steps, rows, cols)
    return (grads[0], grads[1], misfit)


def solution(mesh):
    in_specs = (
        P(None, "gy", "gx"),
        P(None, None, "gy", "gx"),
        P(None, "gy", "gx"),
        P("gy", "gx"),
        P("gy", "gx"),
        P("gy", "gx"),
        P(None, None, "gy", "gx"),
        P("gy", "gx"),
    )
    out_specs = (P("gy", "gx"), P("gy", "gx"), P())
    return jax.shard_map(
        on_device, mesh=mesh, in_specs=in_specs, out_specs=out_specs, check_vma=False
    )
```

```python
import jax
import jax.numpy as jnp
from jax import lax
from jax.experimental import pallas as pl
from jax.experimental.pallas import tpu as pltpu
from jax.sharding import PartitionSpec as P

EPSILON = 1e-06
HALO = 12
LANES = 128


def wrapped_patch(block, width):
    pieces = {}
    for axis, dim in (("gy", 1), ("gx", 2)):
        count = lax.axis_size(axis)
        forward = [(i, i + 1) for i in range(count - 1)]
        backward = [(target, source) for source, target in forward]
        before = lax.ppermute(
            lax.slice_in_dim(block, block.shape[dim] - width, None, axis=dim), axis, forward
        )
        after = lax.ppermute(lax.slice_in_dim(block, 0, width, axis=dim), axis, backward)
        if dim == 1:
            block = jnp.concatenate([block, after, before], axis=dim)
        else:
            lanes = -(-(block.shape[2] + 2 * width) // LANES) * LANES
            gap = jnp.zeros(block.shape[:2] + (lanes - block.shape[2] - 2 * width,), block.dtype)
            block = jnp.concatenate([block, after, gap, before], axis=dim)
    return block


def butterfly_sum(values, axes):
    for axis in axes:
        count = lax.axis_size(axis)
        if count & (count - 1):
            values = lax.psum(values, axis)
            continue
        stride = 1
        while stride < count:
            values = values + lax.ppermute(values, axis, [(i, i ^ stride) for i in range(count)])
            stride *= 2
    return values


SWEEPS = 3
RELAXATION = 0.8
TIME_STEP = 0.1


def make_nb(roll):
    def nb(x, dr, dc):
        if dr:
            x = roll(x, (-dr) % x.shape[0], 0)
        if dc:
            x = roll(x, (-dc) % x.shape[1], 1)
        return x

    return nb


def edges(nb, u, v, h, cov, dr, dc):
    du = nb(u, dr, dc) - u
    dv = nb(v, dr, dc) - v
    s = du * du + dv * dv
    p = jnp.exp(jnp.log(1.0 + s) * (-1.0 / 3.0))
    a = 0.5 * (h + nb(h, dr, dc)) * cov * nb(cov, dr, dc)
    return du, dv, s, p, a, a * p


def sweep_terms(nb, u, v, h, cov, fric, fu, fv):
    de = edges(nb, u, v, h, cov, 0, 1)
    ds = edges(nb, u, v, h, cov, 1, 0)
    ce, cs = de[5], ds[5]
    fe_u, fe_v = ce * de[0], ce * de[1]
    fs_u, fs_v = cs * ds[0], cs * ds[1]
    flux_u = fe_u + fs_u - nb(fe_u, 0, -1) - nb(fs_u, -1, 0)
    flux_v = fe_v + fs_v - nb(fe_v, 0, -1) - nb(fs_v, -1, 0)
    c_sum = ce + cs + nb(ce, 0, -1) + nb(cs, -1, 0)
    r_u = fu - fric * u + flux_u
    r_v = fv - fric * v + flux_v
    d = 1.0 + fric + c_sum
    return de, ds, r_u, r_v, d


def sweep_fwd(nb, u, v, h, cov, fric, fu, fv):
    de, ds, r_u, r_v, d = sweep_terms(nb, u, v, h, cov, fric, fu, fv)
    return cov * (u + RELAXATION * r_u / d), cov * (v + RELAXATION * r_v / d)


def sweep_bwd(nb, u, v, h, cov, fric, su, sv, bu, bv):
    de, ds, r_u, r_v, d = sweep_terms(nb, u, v, h, cov, fric, h * su, h * sv)
    qu, qv = cov * bu, cov * bv
    tu, tv = RELAXATION * qu / d, RELAXATION * qv / d
    d_bar = -(tu * r_u + tv * r_v) / d
    f_bar = d_bar - (tu * u + tv * v)
    h_bar = tu * su + tv * sv
    wu = qu - fric * tu
    wv = qv - fric * tv
    for (du, dv, s, p, a, c), (dr, dc) in ((de, (0, 1)), (ds, (1, 0))):
        big_u = tu - nb(tu, dr, dc)
        big_v = tv - nb(tv, dr, dc)
        c_bar = big_u * du + big_v * dv + d_bar + nb(d_bar, dr, dc)
        a_bar = c_bar * p
        s_bar = c_bar * a * (-1.0 / 3.0) * p / (1.0 + s)
        gu = big_u * c + 2.0 * s_bar * du
        gv = big_v * c + 2.0 * s_bar * dv
        wu = wu - gu + nb(gu, -dr, -dc)
        wv = wv - gv + nb(gv, -dr, -dc)
        k = 0.5 * cov * nb(cov, dr, dc) * a_bar
        h_bar = h_bar + k + nb(k, -dr, -dc)
    return wu, wv, h_bar, f_bar


def transport_bwd(nb, u, v, h, cov, don_e, don_s, g):
    q = cov * g
    h_bar = q
    div_bar = -TIME_STEP * q
    u_bar = None
    v_bar = None
    for vel, don, (dr, dc) in ((u, don_e, (0, 1)), (v, don_s, (1, 0))):
        f_bar = div_bar - nb(div_bar, dr, dc)
        kk = cov * nb(cov, dr, dc)
        speed = 0.5 * (vel + nb(vel, dr, dc))
        hh = don * h + (1.0 - don) * nb(h, dr, dc)
        x = 0.5 * f_bar * kk * hh
        vb = x + nb(x, -dr, -dc)
        y = f_bar * speed * kk
        h_bar = h_bar + y * don + nb(y * (1.0 - don), -dr, -dc)
        if u_bar is None:
            u_bar = vb
        else:
            v_bar = vb
    return u_bar, v_bar, h_bar


def statics(f):
    mask = f["mask"]
    cov = (mask > 0.5).astype(jnp.float32)
    grounded = (mask > 1.5).astype(jnp.float32)
    flags = f["flags"]
    don_s = (flags > 1.5).astype(jnp.float32)
    don_e = flags - 2.0 * don_s
    fric = f["beta"] * grounded
    return cov, grounded, don_e, don_s, fric


def forward_all(nb, f, steps):
    cov, grounded, don_e, don_s, fric = statics(f)
    out = []
    for n in range(steps):
        h = f["thick"][n]
        u, v = f["vel"][n]
        fu, fv = h * f["slope"][0], h * f["slope"][1]
        states = []
        for _ in range(SWEEPS):
            u, v = sweep_fwd(nb, u, v, h, cov, fric, fu, fv)
            states.append((u, v))
        out.append(states)
    return out


def backward_all(nb, f, steps, scales, g, saved):
    cov, grounded, don_e, don_s, fric = statics(f)
    su, sv = f["slope"][0], f["slope"][1]
    beta = jnp.zeros_like(g)
    for n in reversed(range(steps)):
        h = f["thick"][n]
        states = [f["vel"][n]] + [saved(n, k) for k in range(SWEEPS - 1)]
        u, v = saved(n, SWEEPS - 1)
        ou, ov = f["obs"][n]
        inv = 1.0 / scales[n]
        bu, bv, h_bar = transport_bwd(nb, u, v, h, cov, don_e, don_s, g)
        bu = bu + grounded * (u - ou) * inv
        bv = bv + grounded * (v - ov) * inv
        f_tot = jnp.zeros_like(g)
        for k in reversed(range(SWEEPS)):
            wu, wv = states[k]
            bu, bv, hb, fb = sweep_bwd(nb, wu, wv, h, cov, fric, su, sv, bu, bv)
            h_bar = h_bar + hb
            f_tot = f_tot + fb
        beta = beta + grounded * f_tot
        g = h_bar
    return beta, g


def unpack(arr, steps):
    return {
        "mask": arr[0],
        "flags": arr[1],
        "beta": arr[2],
        "slope": (arr[3], arr[4]),
        "thick": [arr[5 + n] for n in range(steps)],
        "vel": [(arr[5 + steps + 2 * n], arr[6 + steps + 2 * n]) for n in range(steps)],
        "obs": [(arr[5 + 3 * steps + 2 * n], arr[6 + 3 * steps + 2 * n]) for n in range(steps)],
        "adj": arr[5 + 5 * steps],
    }


class RefLoader:
    def __init__(self, ref, steps):
        self.ref = ref
        self.steps = steps

    def __getitem__(self, key):
        r, steps = self.ref, self.steps
        if key == "mask":
            return r[0]
        if key == "flags":
            return r[1]
        if key == "beta":
            return r[2]
        if key == "slope":
            return (r[3], r[4])
        if key == "thick":
            return [r[5 + n] for n in range(steps)]
        if key == "vel":
            return [(r[5 + steps + 2 * n], r[6 + steps + 2 * n]) for n in range(steps)]
        if key == "obs":
            return [(r[5 + 3 * steps + 2 * n], r[6 + 3 * steps + 2 * n]) for n in range(steps)]
        if key == "adj":
            return r[5 + 5 * steps]
        raise KeyError(key)


def forward_kernel(steps, rows, cols):
    def kernel(f_ref, o_ref, w_ref):
        nb = make_nb(pltpu.roll)
        loader = RefLoader(f_ref, steps)
        out = forward_all(nb, loader, steps)
        for n, states in enumerate(out):
            for k, (u, v) in enumerate(states):
                w_ref[2 * (n * SWEEPS + k)] = u
                w_ref[2 * (n * SWEEPS + k) + 1] = v
        grounded = (loader["mask"][:rows, :cols] > 1.5).astype(jnp.float32)

        def total(x):
            return jnp.broadcast_to(jnp.sum(jnp.sum(x, axis=0, keepdims=True), axis=1, keepdims=True), o_ref.shape[1:])

        for n, states in enumerate(out):
            u, v = states[-1]
            ou, ov = loader["obs"][n]
            ou, ov = ou[:rows, :cols], ov[:rows, :cols]
            du, dv = u[:rows, :cols] - ou, v[:rows, :cols] - ov
            o_ref[n] = total(grounded * (ou * ou + ov * ov))
            o_ref[steps + n] = total(0.5 * grounded * (du * du + dv * dv))

    return kernel


def backward_kernel(steps, rows, cols):
    def kernel(s_ref, f_ref, w_ref, beta_ref, g_ref):
        nb = make_nb(pltpu.roll)
        loader = RefLoader(f_ref, steps)
        scales = [s_ref[n] for n in range(steps)]

        def saved(n, k):
            return w_ref[2 * (n * SWEEPS + k)], w_ref[2 * (n * SWEEPS + k) + 1]

        beta, g = backward_all(nb, loader, steps, scales, loader["adj"], saved)
        beta_ref[...] = beta[:rows, :cols]
        g_ref[...] = g[:rows, :cols]

    return kernel


def pack_kernel(steps):
    def kernel(thick_ref, vel_ref, slope_ref, beta_ref, mask_ref, flags_ref, obs_ref, adj_ref, o_ref):
        f32 = jnp.float32
        o_ref[0] = mask_ref[...].astype(f32)
        o_ref[1] = flags_ref[...].astype(f32)
        o_ref[2] = beta_ref[...]
        for c in range(2):
            o_ref[3 + c] = slope_ref[c].astype(f32)
        for n in range(steps):
            o_ref[5 + n] = thick_ref[n].astype(f32)
            for c in range(2):
                o_ref[5 + steps + 2 * n + c] = vel_ref[n, c].astype(f32)
                o_ref[5 + 3 * steps + 2 * n + c] = obs_ref[n, c].astype(f32)
        o_ref[5 + 5 * steps] = adj_ref[...]

    return kernel


def run_pack(*arrays):
    steps, rows, cols = arrays[0].shape
    return pl.pallas_call(
        pack_kernel(steps),
        out_shape=jax.ShapeDtypeStruct((6 + 5 * steps, rows, cols), jnp.float32),
        in_specs=[pl.BlockSpec(memory_space=pltpu.VMEM)] * len(arrays),
        out_specs=pl.BlockSpec(memory_space=pltpu.VMEM),
    )(*arrays)


def run_forward(fields, steps, rows, cols):
    _, patch_rows, patch_cols = fields.shape
    return pl.pallas_call(
        forward_kernel(steps, rows, cols),
        out_shape=(
            jax.ShapeDtypeStruct((2 * steps, 8, LANES), jnp.float32),
            jax.ShapeDtypeStruct((2 * SWEEPS * steps, patch_rows, patch_cols), jnp.float32),
        ),
        in_specs=[pl.BlockSpec(memory_space=pltpu.VMEM)],
        out_specs=(pl.BlockSpec(memory_space=pltpu.VMEM),) * 2,
    )(fields)


def run_backward(scales, fields, states, steps, rows, cols):
    return pl.pallas_call(
        backward_kernel(steps, rows, cols),
        out_shape=(jax.ShapeDtypeStruct((rows, cols), jnp.float32),) * 2,
        in_specs=[pl.BlockSpec(memory_space=pltpu.SMEM)] + [pl.BlockSpec(memory_space=pltpu.VMEM)] * 2,
        out_specs=(pl.BlockSpec(memory_space=pltpu.VMEM),) * 2,
    )(scales, fields, states)


def on_device(
    saved_thickness,
    saved_velocity,
    surface_slope,
    basal_beta,
    cell_mask,
    upwind_flags,
    observed_velocity,
    thickness_adjoint,
):
    steps = saved_thickness.shape[0]
    rows, cols = basal_beta.shape
    f32 = jnp.float32
    fields = run_pack(
        saved_thickness,
        saved_velocity,
        surface_slope,
        basal_beta,
        cell_mask,
        upwind_flags,
        observed_velocity,
        thickness_adjoint,
    )
    wide = wrapped_patch(fields, HALO)
    sums, states = run_forward(wide, steps, rows, cols)
    local_sums = sums[:, 0, 0]
    totals = butterfly_sum(local_sums, ("gx", "gy"))
    cell_count = rows * cols * lax.axis_size("gy") * lax.axis_size("gx")
    scales = totals[:steps] / cell_count + EPSILON
    misfit = jnp.zeros((), f32)
    for n in reversed(range(steps)):
        misfit = misfit + totals[steps + n] / cell_count / scales[n]
    grads = run_backward(scales, wide, states, steps, rows, cols)
    return (grads[0], grads[1], misfit)


def solution(mesh):
    in_specs = (
        P(None, "gy", "gx"),
        P(None, None, "gy", "gx"),
        P(None, "gy", "gx"),
        P("gy", "gx"),
        P("gy", "gx"),
        P("gy", "gx"),
        P(None, None, "gy", "gx"),
        P("gy", "gx"),
    )
    out_specs = (P("gy", "gx"), P("gy", "gx"), P())
    return jax.shard_map(
        on_device, mesh=mesh, in_specs=in_specs, out_specs=out_specs, check_vma=False
    )
```

```python
import jax
import jax.numpy as jnp
from jax import lax
from jax.experimental import pallas as pl
from jax.experimental.pallas import tpu as pltpu
from jax.sharding import PartitionSpec as P

EPSILON = 1e-06
HALO = 12
LANES = 128


def wrapped_patch(block, width):
    pieces = {}
    for axis, dim in (("gy", 1), ("gx", 2)):
        count = lax.axis_size(axis)
        forward = [(i, i + 1) for i in range(count - 1)]
        backward = [(target, source) for source, target in forward]
        before = lax.ppermute(
            lax.slice_in_dim(block, block.shape[dim] - width, None, axis=dim), axis, forward
        )
        after = lax.ppermute(lax.slice_in_dim(block, 0, width, axis=dim), axis, backward)
        if dim == 1:
            block = jnp.concatenate([block, after, before], axis=dim)
        else:
            lanes = -(-(block.shape[2] + 2 * width) // LANES) * LANES
            gap = jnp.zeros(block.shape[:2] + (lanes - block.shape[2] - 2 * width,), block.dtype)
            block = jnp.concatenate([block, after, gap, before], axis=dim)
    return block


def butterfly_sum(values, axes):
    for axis in axes:
        count = lax.axis_size(axis)
        if count & (count - 1):
            values = lax.psum(values, axis)
            continue
        stride = 1
        while stride < count:
            values = values + lax.ppermute(values, axis, [(i, i ^ stride) for i in range(count)])
            stride *= 2
    return values


SWEEPS = 3
RELAXATION = 0.8
TIME_STEP = 0.1


def make_nb(roll):
    def nb(x, dr, dc):
        if dr:
            x = roll(x, (-dr) % x.shape[0], 0)
        if dc:
            x = roll(x, (-dc) % x.shape[1], 1)
        return x

    return nb


def edges(nb, u, v, h, cov, dr, dc):
    du = nb(u, dr, dc) - u
    dv = nb(v, dr, dc) - v
    s = du * du + dv * dv
    p = jnp.exp(jnp.log(1.0 + s) * (-1.0 / 3.0))
    a = 0.5 * (h + nb(h, dr, dc)) * cov * nb(cov, dr, dc)
    return du, dv, s, p, a, a * p


def sweep_terms(nb, u, v, h, cov, fric, fu, fv):
    de = edges(nb, u, v, h, cov, 0, 1)
    ds = edges(nb, u, v, h, cov, 1, 0)
    ce, cs = de[5], ds[5]
    fe_u, fe_v = ce * de[0], ce * de[1]
    fs_u, fs_v = cs * ds[0], cs * ds[1]
    flux_u = fe_u + fs_u - nb(fe_u, 0, -1) - nb(fs_u, -1, 0)
    flux_v = fe_v + fs_v - nb(fe_v, 0, -1) - nb(fs_v, -1, 0)
    c_sum = ce + cs + nb(ce, 0, -1) + nb(cs, -1, 0)
    r_u = fu - fric * u + flux_u
    r_v = fv - fric * v + flux_v
    d = 1.0 + fric + c_sum
    return de, ds, r_u, r_v, d


def sweep_fwd(nb, u, v, h, cov, fric, fu, fv):
    de, ds, r_u, r_v, d = sweep_terms(nb, u, v, h, cov, fric, fu, fv)
    return cov * (u + RELAXATION * r_u / d), cov * (v + RELAXATION * r_v / d)


def sweep_bwd(nb, u, v, h, cov, fric, su, sv, bu, bv):
    de, ds, r_u, r_v, d = sweep_terms(nb, u, v, h, cov, fric, h * su, h * sv)
    qu, qv = cov * bu, cov * bv
    tu, tv = RELAXATION * qu / d, RELAXATION * qv / d
    d_bar = -(tu * r_u + tv * r_v) / d
    f_bar = d_bar - (tu * u + tv * v)
    h_bar = tu * su + tv * sv
    wu = qu - fric * tu
    wv = qv - fric * tv
    for (du, dv, s, p, a, c), (dr, dc) in ((de, (0, 1)), (ds, (1, 0))):
        big_u = tu - nb(tu, dr, dc)
        big_v = tv - nb(tv, dr, dc)
        c_bar = big_u * du + big_v * dv + d_bar + nb(d_bar, dr, dc)
        a_bar = c_bar * p
        s_bar = c_bar * a * (-1.0 / 3.0) * p / (1.0 + s)
        gu = big_u * c + 2.0 * s_bar * du
        gv = big_v * c + 2.0 * s_bar * dv
        wu = wu - gu + nb(gu, -dr, -dc)
        wv = wv - gv + nb(gv, -dr, -dc)
        k = 0.5 * cov * nb(cov, dr, dc) * a_bar
        h_bar = h_bar + k + nb(k, -dr, -dc)
    return wu, wv, h_bar, f_bar


def transport_bwd(nb, u, v, h, cov, don_e, don_s, g):
    q = cov * g
    h_bar = q
    div_bar = -TIME_STEP * q
    u_bar = None
    v_bar = None
    for vel, don, (dr, dc) in ((u, don_e, (0, 1)), (v, don_s, (1, 0))):
        f_bar = div_bar - nb(div_bar, dr, dc)
        kk = cov * nb(cov, dr, dc)
        speed = 0.5 * (vel + nb(vel, dr, dc))
        hh = don * h + (1.0 - don) * nb(h, dr, dc)
        x = 0.5 * f_bar * kk * hh
        vb = x + nb(x, -dr, -dc)
        y = f_bar * speed * kk
        h_bar = h_bar + y * don + nb(y * (1.0 - don), -dr, -dc)
        if u_bar is None:
            u_bar = vb
        else:
            v_bar = vb
    return u_bar, v_bar, h_bar


def statics(f):
    mask = f["mask"]
    cov = (mask > 0.5).astype(jnp.float32)
    grounded = (mask > 1.5).astype(jnp.float32)
    flags = f["flags"]
    don_s = (flags > 1.5).astype(jnp.float32)
    don_e = flags - 2.0 * don_s
    fric = f["beta"] * grounded
    return cov, grounded, don_e, don_s, fric


def forward_all(nb, f, steps):
    cov, grounded, don_e, don_s, fric = statics(f)
    out = []
    for n in range(steps):
        h = f["thick"][n]
        u, v = f["vel"][n]
        fu, fv = h * f["slope"][0], h * f["slope"][1]
        for _ in range(SWEEPS):
            u, v = sweep_fwd(nb, u, v, h, cov, fric, fu, fv)
        out.append((u, v))
    return out


def backward_all(nb, f, steps, scales, g):
    cov, grounded, don_e, don_s, fric = statics(f)
    su, sv = f["slope"][0], f["slope"][1]
    beta = jnp.zeros_like(g)
    for n in reversed(range(steps)):
        h = f["thick"][n]
        u, v = f["vel"][n]
        fu, fv = h * su, h * sv
        states = []
        for _ in range(SWEEPS):
            states.append((u, v))
            u, v = sweep_fwd(nb, u, v, h, cov, fric, fu, fv)
        ou, ov = f["obs"][n]
        inv = 1.0 / scales[n]
        bu, bv, h_bar = transport_bwd(nb, u, v, h, cov, don_e, don_s, g)
        bu = bu + grounded * (u - ou) * inv
        bv = bv + grounded * (v - ov) * inv
        f_tot = jnp.zeros_like(g)
        for k in reversed(range(SWEEPS)):
            wu, wv = states[k]
            bu, bv, hb, fb = sweep_bwd(nb, wu, wv, h, cov, fric, su, sv, bu, bv)
            h_bar = h_bar + hb
            f_tot = f_tot + fb
        beta = beta + grounded * f_tot
        g = h_bar
    return beta, g


def unpack(arr, steps):
    return {
        "mask": arr[0],
        "flags": arr[1],
        "beta": arr[2],
        "slope": (arr[3], arr[4]),
        "thick": [arr[5 + n] for n in range(steps)],
        "vel": [(arr[5 + steps + 2 * n], arr[6 + steps + 2 * n]) for n in range(steps)],
        "obs": [(arr[5 + 3 * steps + 2 * n], arr[6 + 3 * steps + 2 * n]) for n in range(steps)],
        "adj": arr[5 + 5 * steps],
    }


class RefLoader:
    def __init__(self, ref, steps):
        self.ref = ref
        self.steps = steps

    def __getitem__(self, key):
        r, steps = self.ref, self.steps
        if key == "mask":
            return r[0]
        if key == "flags":
            return r[1]
        if key == "beta":
            return r[2]
        if key == "slope":
            return (r[3], r[4])
        if key == "thick":
            return [r[5 + n] for n in range(steps)]
        if key == "vel":
            return [(r[5 + steps + 2 * n], r[6 + steps + 2 * n]) for n in range(steps)]
        if key == "obs":
            return [(r[5 + 3 * steps + 2 * n], r[6 + 3 * steps + 2 * n]) for n in range(steps)]
        if key == "adj":
            return r[5 + 5 * steps]
        raise KeyError(key)


def forward_kernel(steps, rows, cols):
    def kernel(f_ref, o_ref):
        nb = make_nb(pltpu.roll)
        loader = RefLoader(f_ref, steps)
        out = forward_all(nb, loader, steps)
        grounded = (loader["mask"][:rows, :cols] > 1.5).astype(jnp.float32)

        def total(x):
            return jnp.sum(x)

        for n, (u, v) in enumerate(out):
            ou, ov = loader["obs"][n]
            ou, ov = ou[:rows, :cols], ov[:rows, :cols]
            du, dv = u[:rows, :cols] - ou, v[:rows, :cols] - ov
            o_ref[n] = total(grounded * (ou * ou + ov * ov))
            o_ref[steps + n] = total(0.5 * grounded * (du * du + dv * dv))

    return kernel


def backward_kernel(steps, rows, cols, cell_count):
    def kernel(s_ref, f_ref, beta_ref, g_ref, m_ref):
        nb = make_nb(pltpu.roll)
        loader = RefLoader(f_ref, steps)
        scales = [s_ref[n] / cell_count + EPSILON for n in range(steps)]
        misfit = s_ref[2 * steps - 1] / cell_count / scales[steps - 1]
        for n in reversed(range(steps - 1)):
            misfit = misfit + s_ref[steps + n] / cell_count / scales[n]
        m_ref[0] = misfit
        beta, g = backward_all(nb, loader, steps, scales, loader["adj"])
        beta_ref[...] = beta[:rows, :cols]
        g_ref[...] = g[:rows, :cols]

    return kernel


def pack_kernel(steps):
    def kernel(thick_ref, vel_ref, slope_ref, beta_ref, mask_ref, flags_ref, obs_ref, adj_ref, o_ref):
        f32 = jnp.float32
        o_ref[0] = mask_ref[...].astype(f32)
        o_ref[1] = flags_ref[...].astype(f32)
        o_ref[2] = beta_ref[...]
        for c in range(2):
            o_ref[3 + c] = slope_ref[c].astype(f32)
        for n in range(steps):
            o_ref[5 + n] = thick_ref[n].astype(f32)
            for c in range(2):
                o_ref[5 + steps + 2 * n + c] = vel_ref[n, c].astype(f32)
                o_ref[5 + 3 * steps + 2 * n + c] = obs_ref[n, c].astype(f32)
        o_ref[5 + 5 * steps] = adj_ref[...]

    return kernel


def run_pack(*arrays):
    steps, rows, cols = arrays[0].shape
    return pl.pallas_call(
        pack_kernel(steps),
        out_shape=jax.ShapeDtypeStruct((6 + 5 * steps, rows, cols), jnp.float32),
        in_specs=[pl.BlockSpec(memory_space=pltpu.VMEM)] * len(arrays),
        out_specs=pl.BlockSpec(memory_space=pltpu.VMEM),
    )(*arrays)


def run_forward(fields, steps, rows, cols):
    return pl.pallas_call(
        forward_kernel(steps, rows, cols),
        out_shape=jax.ShapeDtypeStruct((2 * steps,), jnp.float32),
        in_specs=[pl.BlockSpec(memory_space=pltpu.VMEM)],
        out_specs=pl.BlockSpec(memory_space=pltpu.SMEM),
    )(fields)


def run_backward(totals, fields, steps, rows, cols, cell_count):
    return pl.pallas_call(
        backward_kernel(steps, rows, cols, cell_count),
        out_shape=(jax.ShapeDtypeStruct((rows, cols), jnp.float32),) * 2
        + (jax.ShapeDtypeStruct((1,), jnp.float32),),
        in_specs=[pl.BlockSpec(memory_space=pltpu.SMEM), pl.BlockSpec(memory_space=pltpu.VMEM)],
        out_specs=(pl.BlockSpec(memory_space=pltpu.VMEM),) * 2 + (pl.BlockSpec(memory_space=pltpu.SMEM),),
    )(totals, fields)


def on_device(
    saved_thickness,
    saved_velocity,
    surface_slope,
    basal_beta,
    cell_mask,
    upwind_flags,
    observed_velocity,
    thickness_adjoint,
):
    steps = saved_thickness.shape[0]
    rows, cols = basal_beta.shape
    f32 = jnp.float32
    fields = run_pack(
        saved_thickness,
        saved_velocity,
        surface_slope,
        basal_beta,
        cell_mask,
        upwind_flags,
        observed_velocity,
        thickness_adjoint,
    )
    wide = wrapped_patch(fields, HALO)
    local_sums = run_forward(wide, steps, rows, cols)
    totals = butterfly_sum(local_sums, ("gx", "gy"))
    cell_count = rows * cols * lax.axis_size("gy") * lax.axis_size("gx")
    beta_gradient, thickness_gradient, misfit = run_backward(totals, wide, steps, rows, cols, cell_count)
    return (beta_gradient, thickness_gradient, misfit.reshape(()))


def solution(mesh):
    in_specs = (
        P(None, "gy", "gx"),
        P(None, None, "gy", "gx"),
        P(None, "gy", "gx"),
        P("gy", "gx"),
        P("gy", "gx"),
        P("gy", "gx"),
        P(None, None, "gy", "gx"),
        P("gy", "gx"),
    )
    out_specs = (P("gy", "gx"), P("gy", "gx"), P())
    return jax.shard_map(
        on_device, mesh=mesh, in_specs=in_specs, out_specs=out_specs, check_vma=False
    )
```

```python
import jax
import jax.numpy as jnp
from jax import lax
from jax.experimental import pallas as pl
from jax.experimental.pallas import tpu as pltpu
from jax.sharding import PartitionSpec as P

EPSILON = 1e-06
HALO = 12
LANES = 128


def wrapped_patch(block, width, first_rows, last_rows):
    pieces = {}
    for axis, dim in (("gy", 1), ("gx", 2)):
        count = lax.axis_size(axis)
        forward = [(i, i + 1) for i in range(count - 1)]
        backward = [(target, source) for source, target in forward]
        if dim == 1:
            before = lax.ppermute(last_rows, axis, forward)
            after = lax.ppermute(first_rows, axis, backward)
        else:
            before = lax.ppermute(
                lax.slice_in_dim(block, block.shape[dim] - width, None, axis=dim), axis, forward
            )
            after = lax.ppermute(lax.slice_in_dim(block, 0, width, axis=dim), axis, backward)
        if dim == 1:
            block = jnp.concatenate([block, after, before], axis=dim)
        else:
            lanes = -(-(block.shape[2] + 2 * width) // LANES) * LANES
            gap = jnp.zeros(block.shape[:2] + (lanes - block.shape[2] - 2 * width,), block.dtype)
            block = jnp.concatenate([block, after, gap, before], axis=dim)
    return block


def butterfly_sum(values, axes):
    for axis in axes:
        count = lax.axis_size(axis)
        if count & (count - 1):
            values = lax.psum(values, axis)
            continue
        stride = 1
        while stride < count:
            values = values + lax.ppermute(values, axis, [(i, i ^ stride) for i in range(count)])
            stride *= 2
    return values


SWEEPS = 3
RELAXATION = 0.8
TIME_STEP = 0.1


def make_nb(roll):
    def nb(x, dr, dc):
        if dr:
            x = roll(x, (-dr) % x.shape[0], 0)
        if dc:
            x = roll(x, (-dc) % x.shape[1], 1)
        return x

    return nb


def edges(nb, u, v, h, cov, dr, dc):
    du = nb(u, dr, dc) - u
    dv = nb(v, dr, dc) - v
    s = du * du + dv * dv
    p = jnp.exp(jnp.log(1.0 + s) * (-1.0 / 3.0))
    a = 0.5 * (h + nb(h, dr, dc)) * cov * nb(cov, dr, dc)
    return du, dv, s, p, a, a * p


def sweep_terms(nb, u, v, h, cov, fric, fu, fv):
    de = edges(nb, u, v, h, cov, 0, 1)
    ds = edges(nb, u, v, h, cov, 1, 0)
    ce, cs = de[5], ds[5]
    fe_u, fe_v = ce * de[0], ce * de[1]
    fs_u, fs_v = cs * ds[0], cs * ds[1]
    flux_u = fe_u + fs_u - nb(fe_u, 0, -1) - nb(fs_u, -1, 0)
    flux_v = fe_v + fs_v - nb(fe_v, 0, -1) - nb(fs_v, -1, 0)
    c_sum = ce + cs + nb(ce, 0, -1) + nb(cs, -1, 0)
    r_u = fu - fric * u + flux_u
    r_v = fv - fric * v + flux_v
    d = 1.0 + fric + c_sum
    return de, ds, r_u, r_v, d


def sweep_fwd(nb, u, v, h, cov, fric, fu, fv):
    de, ds, r_u, r_v, d = sweep_terms(nb, u, v, h, cov, fric, fu, fv)
    return cov * (u + RELAXATION * r_u / d), cov * (v + RELAXATION * r_v / d)


def sweep_bwd(nb, u, v, h, cov, fric, su, sv, bu, bv):
    de, ds, r_u, r_v, d = sweep_terms(nb, u, v, h, cov, fric, h * su, h * sv)
    qu, qv = cov * bu, cov * bv
    tu, tv = RELAXATION * qu / d, RELAXATION * qv / d
    d_bar = -(tu * r_u + tv * r_v) / d
    f_bar = d_bar - (tu * u + tv * v)
    h_bar = tu * su + tv * sv
    wu = qu - fric * tu
    wv = qv - fric * tv
    for (du, dv, s, p, a, c), (dr, dc) in ((de, (0, 1)), (ds, (1, 0))):
        big_u = tu - nb(tu, dr, dc)
        big_v = tv - nb(tv, dr, dc)
        c_bar = big_u * du + big_v * dv + d_bar + nb(d_bar, dr, dc)
        a_bar = c_bar * p
        s_bar = c_bar * a * (-1.0 / 3.0) * p / (1.0 + s)
        gu = big_u * c + 2.0 * s_bar * du
        gv = big_v * c + 2.0 * s_bar * dv
        wu = wu - gu + nb(gu, -dr, -dc)
        wv = wv - gv + nb(gv, -dr, -dc)
        k = 0.5 * cov * nb(cov, dr, dc) * a_bar
        h_bar = h_bar + k + nb(k, -dr, -dc)
    return wu, wv, h_bar, f_bar


def transport_bwd(nb, u, v, h, cov, don_e, don_s, g):
    q = cov * g
    h_bar = q
    div_bar = -TIME_STEP * q
    u_bar = None
    v_bar = None
    for vel, don, (dr, dc) in ((u, don_e, (0, 1)), (v, don_s, (1, 0))):
        f_bar = div_bar - nb(div_bar, dr, dc)
        kk = cov * nb(cov, dr, dc)
        speed = 0.5 * (vel + nb(vel, dr, dc))
        hh = don * h + (1.0 - don) * nb(h, dr, dc)
        x = 0.5 * f_bar * kk * hh
        vb = x + nb(x, -dr, -dc)
        y = f_bar * speed * kk
        h_bar = h_bar + y * don + nb(y * (1.0 - don), -dr, -dc)
        if u_bar is None:
            u_bar = vb
        else:
            v_bar = vb
    return u_bar, v_bar, h_bar


def statics(f):
    mask = f["mask"]
    cov = (mask > 0.5).astype(jnp.float32)
    grounded = (mask > 1.5).astype(jnp.float32)
    flags = f["flags"]
    don_s = (flags > 1.5).astype(jnp.float32)
    don_e = flags - 2.0 * don_s
    fric = f["beta"] * grounded
    return cov, grounded, don_e, don_s, fric


def forward_all(nb, f, steps):
    cov, grounded, don_e, don_s, fric = statics(f)
    out = []
    for n in range(steps):
        h = f["thick"][n]
        u, v = f["vel"][n]
        fu, fv = h * f["slope"][0], h * f["slope"][1]
        for _ in range(SWEEPS):
            u, v = sweep_fwd(nb, u, v, h, cov, fric, fu, fv)
        out.append((u, v))
    return out


def backward_all(nb, f, steps, scales, g):
    cov, grounded, don_e, don_s, fric = statics(f)
    su, sv = f["slope"][0], f["slope"][1]
    beta = jnp.zeros_like(g)
    for n in reversed(range(steps)):
        h = f["thick"][n]
        u, v = f["vel"][n]
        fu, fv = h * su, h * sv
        states = []
        for _ in range(SWEEPS):
            states.append((u, v))
            u, v = sweep_fwd(nb, u, v, h, cov, fric, fu, fv)
        ou, ov = f["obs"][n]
        inv = 1.0 / scales[n]
        bu, bv, h_bar = transport_bwd(nb, u, v, h, cov, don_e, don_s, g)
        bu = bu + grounded * (u - ou) * inv
        bv = bv + grounded * (v - ov) * inv
        f_tot = jnp.zeros_like(g)
        for k in reversed(range(SWEEPS)):
            wu, wv = states[k]
            bu, bv, hb, fb = sweep_bwd(nb, wu, wv, h, cov, fric, su, sv, bu, bv)
            h_bar = h_bar + hb
            f_tot = f_tot + fb
        beta = beta + grounded * f_tot
        g = h_bar
    return beta, g


def unpack(arr, steps):
    return {
        "mask": arr[0],
        "flags": arr[1],
        "beta": arr[2],
        "slope": (arr[3], arr[4]),
        "thick": [arr[5 + n] for n in range(steps)],
        "vel": [(arr[5 + steps + 2 * n], arr[6 + steps + 2 * n]) for n in range(steps)],
        "obs": [(arr[5 + 3 * steps + 2 * n], arr[6 + 3 * steps + 2 * n]) for n in range(steps)],
        "adj": arr[5 + 5 * steps],
    }


class RefLoader:
    def __init__(self, ref, steps):
        self.ref = ref
        self.steps = steps

    def __getitem__(self, key):
        r, steps = self.ref, self.steps
        if key == "mask":
            return r[0]
        if key == "flags":
            return r[1]
        if key == "beta":
            return r[2]
        if key == "slope":
            return (r[3], r[4])
        if key == "thick":
            return [r[5 + n] for n in range(steps)]
        if key == "vel":
            return [(r[5 + steps + 2 * n], r[6 + steps + 2 * n]) for n in range(steps)]
        if key == "obs":
            return [(r[5 + 3 * steps + 2 * n], r[6 + 3 * steps + 2 * n]) for n in range(steps)]
        if key == "adj":
            return r[5 + 5 * steps]
        raise KeyError(key)


def forward_kernel(steps, rows, cols):
    def kernel(f_ref, o_ref):
        nb = make_nb(pltpu.roll)
        loader = RefLoader(f_ref, steps)
        out = forward_all(nb, loader, steps)
        grounded = (loader["mask"][:rows, :cols] > 1.5).astype(jnp.float32)

        def total(x):
            return jnp.sum(x)

        for n, (u, v) in enumerate(out):
            ou, ov = loader["obs"][n]
            ou, ov = ou[:rows, :cols], ov[:rows, :cols]
            du, dv = u[:rows, :cols] - ou, v[:rows, :cols] - ov
            o_ref[n] = total(grounded * (ou * ou + ov * ov))
            o_ref[steps + n] = total(0.5 * grounded * (du * du + dv * dv))

    return kernel


def backward_kernel(steps, rows, cols, cell_count):
    def kernel(s_ref, f_ref, beta_ref, g_ref, m_ref):
        nb = make_nb(pltpu.roll)
        loader = RefLoader(f_ref, steps)
        scales = [s_ref[n] / cell_count + EPSILON for n in range(steps)]
        misfit = s_ref[2 * steps - 1] / cell_count / scales[steps - 1]
        for n in reversed(range(steps - 1)):
            misfit = misfit + s_ref[steps + n] / cell_count / scales[n]
        m_ref[0] = misfit
        beta, g = backward_all(nb, loader, steps, scales, loader["adj"])
        beta_ref[...] = beta[:rows, :cols]
        g_ref[...] = g[:rows, :cols]

    return kernel


def pack_kernel(steps):
    def kernel(thick_ref, vel_ref, slope_ref, beta_ref, mask_ref, flags_ref, obs_ref, adj_ref, o_ref, top_ref, bottom_ref):
        f32 = jnp.float32
        o_ref[0] = mask_ref[...].astype(f32)
        o_ref[1] = flags_ref[...].astype(f32)
        o_ref[2] = beta_ref[...]
        for c in range(2):
            o_ref[3 + c] = slope_ref[c].astype(f32)
        for n in range(steps):
            o_ref[5 + n] = thick_ref[n].astype(f32)
            for c in range(2):
                o_ref[5 + steps + 2 * n + c] = vel_ref[n, c].astype(f32)
                o_ref[5 + 3 * steps + 2 * n + c] = obs_ref[n, c].astype(f32)
        o_ref[5 + 5 * steps] = adj_ref[...]
        width = top_ref.shape[1]
        top_ref[...] = o_ref[:, :width, :]
        bottom_ref[...] = o_ref[:, o_ref.shape[1] - width :, :]

    return kernel


def run_pack(width, *arrays):
    steps, rows, cols = arrays[0].shape
    fields = 6 + 5 * steps
    return pl.pallas_call(
        pack_kernel(steps),
        out_shape=(
            jax.ShapeDtypeStruct((fields, rows, cols), jnp.float32),
            jax.ShapeDtypeStruct((fields, width, cols), jnp.float32),
            jax.ShapeDtypeStruct((fields, width, cols), jnp.float32),
        ),
        in_specs=[pl.BlockSpec(memory_space=pltpu.VMEM)] * len(arrays),
        out_specs=(pl.BlockSpec(memory_space=pltpu.VMEM),) * 3,
    )(*arrays)


def run_forward(fields, steps, rows, cols):
    return pl.pallas_call(
        forward_kernel(steps, rows, cols),
        out_shape=jax.ShapeDtypeStruct((2 * steps,), jnp.float32),
        in_specs=[pl.BlockSpec(memory_space=pltpu.VMEM)],
        out_specs=pl.BlockSpec(memory_space=pltpu.SMEM),
    )(fields)


def run_backward(totals, fields, steps, rows, cols, cell_count):
    return pl.pallas_call(
        backward_kernel(steps, rows, cols, cell_count),
        out_shape=(jax.ShapeDtypeStruct((rows, cols), jnp.float32),) * 2
        + (jax.ShapeDtypeStruct((1,), jnp.float32),),
        in_specs=[pl.BlockSpec(memory_space=pltpu.SMEM), pl.BlockSpec(memory_space=pltpu.VMEM)],
        out_specs=(pl.BlockSpec(memory_space=pltpu.VMEM),) * 2 + (pl.BlockSpec(memory_space=pltpu.SMEM),),
    )(totals, fields)


def on_device(
    saved_thickness,
    saved_velocity,
    surface_slope,
    basal_beta,
    cell_mask,
    upwind_flags,
    observed_velocity,
    thickness_adjoint,
):
    steps = saved_thickness.shape[0]
    rows, cols = basal_beta.shape
    f32 = jnp.float32
    fields, first_rows, last_rows = run_pack(
        HALO,
        saved_thickness,
        saved_velocity,
        surface_slope,
        basal_beta,
        cell_mask,
        upwind_flags,
        observed_velocity,
        thickness_adjoint,
    )
    wide = wrapped_patch(fields, HALO, first_rows, last_rows)
    local_sums = run_forward(wide, steps, rows, cols)
    totals = butterfly_sum(local_sums, ("gx", "gy"))
    cell_count = rows * cols * lax.axis_size("gy") * lax.axis_size("gx")
    beta_gradient, thickness_gradient, misfit = run_backward(totals, wide, steps, rows, cols, cell_count)
    return (beta_gradient, thickness_gradient, misfit.reshape(()))


def solution(mesh):
    in_specs = (
        P(None, "gy", "gx"),
        P(None, None, "gy", "gx"),
        P(None, "gy", "gx"),
        P("gy", "gx"),
        P("gy", "gx"),
        P("gy", "gx"),
        P(None, None, "gy", "gx"),
        P("gy", "gx"),
    )
    out_specs = (P("gy", "gx"), P("gy", "gx"), P())
    return jax.shard_map(
        on_device, mesh=mesh, in_specs=in_specs, out_specs=out_specs, check_vma=False
    )
```

```python
import jax
import jax.numpy as jnp
from jax import lax
from jax.experimental import pallas as pl
from jax.experimental.pallas import tpu as pltpu
from jax.sharding import PartitionSpec as P

EPSILON = 1e-06
HALO = 12
LANES = 128


def wrapped_patch(block, width, first_rows, last_rows):
    pieces = {}
    for axis, dim in (("gy", 1), ("gx", 2)):
        count = lax.axis_size(axis)
        forward = [(i, i + 1) for i in range(count - 1)]
        backward = [(target, source) for source, target in forward]
        if dim == 1:
            before = lax.ppermute(last_rows, axis, forward)
            after = lax.ppermute(first_rows, axis, backward)
        else:
            before = lax.ppermute(
                lax.slice_in_dim(block, block.shape[dim] - width, None, axis=dim), axis, forward
            )
            after = lax.ppermute(lax.slice_in_dim(block, 0, width, axis=dim), axis, backward)
        if dim == 1:
            block = jnp.concatenate([block, after, before], axis=dim)
        else:
            lanes = -(-(block.shape[2] + 2 * width) // LANES) * LANES
            gap = jnp.zeros(block.shape[:2] + (lanes - block.shape[2] - 2 * width,), block.dtype)
            block = jnp.concatenate([block, after, gap, before], axis=dim)
    return block


def butterfly_sum(values, axes):
    for axis in axes:
        count = lax.axis_size(axis)
        if count & (count - 1):
            values = lax.psum(values, axis)
            continue
        stride = 1
        while stride < count:
            values = values + lax.ppermute(values, axis, [(i, i ^ stride) for i in range(count)])
            stride *= 2
    return values


def radix_sum(values, axis, radices):
    count = lax.axis_size(axis)
    stride = 1
    for radix in radices:
        digit = (lax.axis_index(axis) // stride) % radix
        received = [values]
        for shift in range(1, radix):
            pairs = []
            for i in range(count):
                own = (i // stride) % radix
                pairs.append((i + (((own + shift) % radix) - own) * stride, i))
            received.append(lax.ppermute(values, axis, pairs))
        stacked = jnp.stack(received)
        ordered = stacked[(jnp.arange(radix) - digit) % radix]
        values = ordered[0]
        for k in range(1, radix):
            values = values + ordered[k]
        stride *= radix
    return values


SWEEPS = 3
RELAXATION = 0.8
TIME_STEP = 0.1


def make_nb(roll):
    def nb(x, dr, dc):
        if dr:
            x = roll(x, (-dr) % x.shape[0], 0)
        if dc:
            x = roll(x, (-dc) % x.shape[1], 1)
        return x

    return nb


def edges(nb, u, v, h, cov, dr, dc):
    du = nb(u, dr, dc) - u
    dv = nb(v, dr, dc) - v
    s = du * du + dv * dv
    p = jnp.exp(jnp.log(1.0 + s) * (-1.0 / 3.0))
    a = 0.5 * (h + nb(h, dr, dc)) * cov * nb(cov, dr, dc)
    return du, dv, s, p, a, a * p


def sweep_terms(nb, u, v, h, cov, fric, fu, fv):
    de = edges(nb, u, v, h, cov, 0, 1)
    ds = edges(nb, u, v, h, cov, 1, 0)
    ce, cs = de[5], ds[5]
    fe_u, fe_v = ce * de[0], ce * de[1]
    fs_u, fs_v = cs * ds[0], cs * ds[1]
    flux_u = fe_u + fs_u - nb(fe_u, 0, -1) - nb(fs_u, -1, 0)
    flux_v = fe_v + fs_v - nb(fe_v, 0, -1) - nb(fs_v, -1, 0)
    c_sum = ce + cs + nb(ce, 0, -1) + nb(cs, -1, 0)
    r_u = fu - fric * u + flux_u
    r_v = fv - fric * v + flux_v
    d = 1.0 + fric + c_sum
    return de, ds, r_u, r_v, d


def sweep_fwd(nb, u, v, h, cov, fric, fu, fv):
    de, ds, r_u, r_v, d = sweep_terms(nb, u, v, h, cov, fric, fu, fv)
    return cov * (u + RELAXATION * r_u / d), cov * (v + RELAXATION * r_v / d)


def sweep_bwd(nb, u, v, h, cov, fric, su, sv, bu, bv):
    de, ds, r_u, r_v, d = sweep_terms(nb, u, v, h, cov, fric, h * su, h * sv)
    qu, qv = cov * bu, cov * bv
    tu, tv = RELAXATION * qu / d, RELAXATION * qv / d
    d_bar = -(tu * r_u + tv * r_v) / d
    f_bar = d_bar - (tu * u + tv * v)
    h_bar = tu * su + tv * sv
    wu = qu - fric * tu
    wv = qv - fric * tv
    for (du, dv, s, p, a, c), (dr, dc) in ((de, (0, 1)), (ds, (1, 0))):
        big_u = tu - nb(tu, dr, dc)
        big_v = tv - nb(tv, dr, dc)
        c_bar = big_u * du + big_v * dv + d_bar + nb(d_bar, dr, dc)
        a_bar = c_bar * p
        s_bar = c_bar * a * (-1.0 / 3.0) * p / (1.0 + s)
        gu = big_u * c + 2.0 * s_bar * du
        gv = big_v * c + 2.0 * s_bar * dv
        wu = wu - gu + nb(gu, -dr, -dc)
        wv = wv - gv + nb(gv, -dr, -dc)
        k = 0.5 * cov * nb(cov, dr, dc) * a_bar
        h_bar = h_bar + k + nb(k, -dr, -dc)
    return wu, wv, h_bar, f_bar


def transport_bwd(nb, u, v, h, cov, don_e, don_s, g):
    q = cov * g
    h_bar = q
    div_bar = -TIME_STEP * q
    u_bar = None
    v_bar = None
    for vel, don, (dr, dc) in ((u, don_e, (0, 1)), (v, don_s, (1, 0))):
        f_bar = div_bar - nb(div_bar, dr, dc)
        kk = cov * nb(cov, dr, dc)
        speed = 0.5 * (vel + nb(vel, dr, dc))
        hh = don * h + (1.0 - don) * nb(h, dr, dc)
        x = 0.5 * f_bar * kk * hh
        vb = x + nb(x, -dr, -dc)
        y = f_bar * speed * kk
        h_bar = h_bar + y * don + nb(y * (1.0 - don), -dr, -dc)
        if u_bar is None:
            u_bar = vb
        else:
            v_bar = vb
    return u_bar, v_bar, h_bar


def statics(f):
    mask = f["mask"]
    cov = (mask > 0.5).astype(jnp.float32)
    grounded = (mask > 1.5).astype(jnp.float32)
    flags = f["flags"]
    don_s = (flags > 1.5).astype(jnp.float32)
    don_e = flags - 2.0 * don_s
    fric = f["beta"] * grounded
    return cov, grounded, don_e, don_s, fric


def forward_all(nb, f, steps):
    cov, grounded, don_e, don_s, fric = statics(f)
    out = []
    for n in range(steps):
        h = f["thick"][n]
        u, v = f["vel"][n]
        fu, fv = h * f["slope"][0], h * f["slope"][1]
        for _ in range(SWEEPS):
            u, v = sweep_fwd(nb, u, v, h, cov, fric, fu, fv)
        out.append((u, v))
    return out


def backward_all(nb, f, steps, scales, g):
    cov, grounded, don_e, don_s, fric = statics(f)
    su, sv = f["slope"][0], f["slope"][1]
    beta = jnp.zeros_like(g)
    for n in reversed(range(steps)):
        h = f["thick"][n]
        u, v = f["vel"][n]
        fu, fv = h * su, h * sv
        states = []
        for _ in range(SWEEPS):
            states.append((u, v))
            u, v = sweep_fwd(nb, u, v, h, cov, fric, fu, fv)
        ou, ov = f["obs"][n]
        inv = 1.0 / scales[n]
        bu, bv, h_bar = transport_bwd(nb, u, v, h, cov, don_e, don_s, g)
        bu = bu + grounded * (u - ou) * inv
        bv = bv + grounded * (v - ov) * inv
        f_tot = jnp.zeros_like(g)
        for k in reversed(range(SWEEPS)):
            wu, wv = states[k]
            bu, bv, hb, fb = sweep_bwd(nb, wu, wv, h, cov, fric, su, sv, bu, bv)
            h_bar = h_bar + hb
            f_tot = f_tot + fb
        beta = beta + grounded * f_tot
        g = h_bar
    return beta, g


def unpack(arr, steps):
    return {
        "mask": arr[0],
        "flags": arr[1],
        "beta": arr[2],
        "slope": (arr[3], arr[4]),
        "thick": [arr[5 + n] for n in range(steps)],
        "vel": [(arr[5 + steps + 2 * n], arr[6 + steps + 2 * n]) for n in range(steps)],
        "obs": [(arr[5 + 3 * steps + 2 * n], arr[6 + 3 * steps + 2 * n]) for n in range(steps)],
        "adj": arr[5 + 5 * steps],
    }


class RefLoader:
    def __init__(self, ref, steps):
        self.ref = ref
        self.steps = steps

    def __getitem__(self, key):
        r, steps = self.ref, self.steps
        if key == "mask":
            return r[0]
        if key == "flags":
            return r[1]
        if key == "beta":
            return r[2]
        if key == "slope":
            return (r[3], r[4])
        if key == "thick":
            return [r[5 + n] for n in range(steps)]
        if key == "vel":
            return [(r[5 + steps + 2 * n], r[6 + steps + 2 * n]) for n in range(steps)]
        if key == "obs":
            return [(r[5 + 3 * steps + 2 * n], r[6 + 3 * steps + 2 * n]) for n in range(steps)]
        if key == "adj":
            return r[5 + 5 * steps]
        raise KeyError(key)


def forward_kernel(steps, rows, cols):
    def kernel(f_ref, o_ref):
        nb = make_nb(pltpu.roll)
        loader = RefLoader(f_ref, steps)
        out = forward_all(nb, loader, steps)
        grounded = (loader["mask"][:rows, :cols] > 1.5).astype(jnp.float32)

        def total(x):
            return jnp.sum(x)

        for n, (u, v) in enumerate(out):
            ou, ov = loader["obs"][n]
            ou, ov = ou[:rows, :cols], ov[:rows, :cols]
            du, dv = u[:rows, :cols] - ou, v[:rows, :cols] - ov
            o_ref[n] = total(grounded * (ou * ou + ov * ov))
            o_ref[steps + n] = total(0.5 * grounded * (du * du + dv * dv))

    return kernel


def backward_kernel(steps, rows, cols, cell_count):
    def kernel(s_ref, f_ref, beta_ref, g_ref, m_ref):
        nb = make_nb(pltpu.roll)
        loader = RefLoader(f_ref, steps)
        scales = [s_ref[n] / cell_count + EPSILON for n in range(steps)]
        misfit = s_ref[2 * steps - 1] / cell_count / scales[steps - 1]
        for n in reversed(range(steps - 1)):
            misfit = misfit + s_ref[steps + n] / cell_count / scales[n]
        m_ref[0] = misfit
        beta, g = backward_all(nb, loader, steps, scales, loader["adj"])
        beta_ref[...] = beta[:rows, :cols]
        g_ref[...] = g[:rows, :cols]

    return kernel


def pack_kernel(steps):
    def kernel(thick_ref, vel_ref, slope_ref, beta_ref, mask_ref, flags_ref, obs_ref, adj_ref, o_ref, top_ref, bottom_ref):
        f32 = jnp.float32
        o_ref[0] = mask_ref[...].astype(f32)
        o_ref[1] = flags_ref[...].astype(f32)
        o_ref[2] = beta_ref[...]
        for c in range(2):
            o_ref[3 + c] = slope_ref[c].astype(f32)
        for n in range(steps):
            o_ref[5 + n] = thick_ref[n].astype(f32)
            for c in range(2):
                o_ref[5 + steps + 2 * n + c] = vel_ref[n, c].astype(f32)
                o_ref[5 + 3 * steps + 2 * n + c] = obs_ref[n, c].astype(f32)
        o_ref[5 + 5 * steps] = adj_ref[...]
        width = top_ref.shape[1]
        top_ref[...] = o_ref[:, :width, :]
        bottom_ref[...] = o_ref[:, o_ref.shape[1] - width :, :]

    return kernel


def run_pack(width, *arrays):
    steps, rows, cols = arrays[0].shape
    fields = 6 + 5 * steps
    return pl.pallas_call(
        pack_kernel(steps),
        out_shape=(
            jax.ShapeDtypeStruct((fields, rows, cols), jnp.float32),
            jax.ShapeDtypeStruct((fields, width, cols), jnp.float32),
            jax.ShapeDtypeStruct((fields, width, cols), jnp.float32),
        ),
        in_specs=[pl.BlockSpec(memory_space=pltpu.VMEM)] * len(arrays),
        out_specs=(pl.BlockSpec(memory_space=pltpu.VMEM),) * 3,
    )(*arrays)


def run_forward(fields, steps, rows, cols):
    return pl.pallas_call(
        forward_kernel(steps, rows, cols),
        out_shape=jax.ShapeDtypeStruct((2 * steps,), jnp.float32),
        in_specs=[pl.BlockSpec(memory_space=pltpu.VMEM)],
        out_specs=pl.BlockSpec(memory_space=pltpu.SMEM),
    )(fields)


def run_backward(totals, fields, steps, rows, cols, cell_count):
    return pl.pallas_call(
        backward_kernel(steps, rows, cols, cell_count),
        out_shape=(jax.ShapeDtypeStruct((rows, cols), jnp.float32),) * 2
        + (jax.ShapeDtypeStruct((1,), jnp.float32),),
        in_specs=[pl.BlockSpec(memory_space=pltpu.SMEM), pl.BlockSpec(memory_space=pltpu.VMEM)],
        out_specs=(pl.BlockSpec(memory_space=pltpu.VMEM),) * 2 + (pl.BlockSpec(memory_space=pltpu.SMEM),),
    )(totals, fields)


def on_device(
    saved_thickness,
    saved_velocity,
    surface_slope,
    basal_beta,
    cell_mask,
    upwind_flags,
    observed_velocity,
    thickness_adjoint,
):
    steps = saved_thickness.shape[0]
    rows, cols = basal_beta.shape
    f32 = jnp.float32
    fields, first_rows, last_rows = run_pack(
        HALO,
        saved_thickness,
        saved_velocity,
        surface_slope,
        basal_beta,
        cell_mask,
        upwind_flags,
        observed_velocity,
        thickness_adjoint,
    )
    wide = wrapped_patch(fields, HALO, first_rows, last_rows)
    local_sums = run_forward(wide, steps, rows, cols)
    if lax.axis_size("gx") == 32 and lax.axis_size("gy") == 8:
        totals = radix_sum(radix_sum(local_sums, "gx", (2, 4, 4)), "gy", (2, 4))
    else:
        totals = butterfly_sum(local_sums, ("gx", "gy"))
    cell_count = rows * cols * lax.axis_size("gy") * lax.axis_size("gx")
    beta_gradient, thickness_gradient, misfit = run_backward(totals, wide, steps, rows, cols, cell_count)
    return (beta_gradient, thickness_gradient, misfit.reshape(()))


def solution(mesh):
    in_specs = (
        P(None, "gy", "gx"),
        P(None, None, "gy", "gx"),
        P(None, "gy", "gx"),
        P("gy", "gx"),
        P("gy", "gx"),
        P("gy", "gx"),
        P(None, None, "gy", "gx"),
        P("gy", "gx"),
    )
    out_specs = (P("gy", "gx"), P("gy", "gx"), P())
    return jax.shard_map(
        on_device, mesh=mesh, in_specs=in_specs, out_specs=out_specs, check_vma=False
    )
```

```python
import jax
import jax.numpy as jnp
from jax import lax
from jax.experimental import pallas as pl
from jax.experimental.pallas import tpu as pltpu
from jax.sharding import PartitionSpec as P

EPSILON = 1e-06
HALO = 12
LANES = 128


def wrapped_patch(block, width, first_rows, last_rows):
    rows_axis = lax.axis_size("gy")
    forward = [(i, i + 1) for i in range(rows_axis - 1)]
    backward = [(target, source) for source, target in forward]
    north = lax.ppermute(last_rows, "gy", forward)
    south = lax.ppermute(first_rows, "gy", backward)
    bands = (block, south, north)
    cols_axis = lax.axis_size("gx")
    forward = [(i, i + 1) for i in range(cols_axis - 1)]
    backward = [(target, source) for source, target in forward]
    cols = block.shape[2]
    west = lax.ppermute(jnp.concatenate([b[..., cols - width :] for b in bands], axis=1), "gx", forward)
    east = lax.ppermute(jnp.concatenate([b[..., :width] for b in bands], axis=1), "gx", backward)
    lanes = -(-(cols + 2 * width) // LANES) * LANES
    middle = jnp.concatenate(bands, axis=1)
    gap = jnp.zeros(middle.shape[:2] + (lanes - cols - 2 * width,), block.dtype)
    return jnp.concatenate([middle, east, gap, west], axis=2)


def butterfly_sum(values, axes):
    for axis in axes:
        count = lax.axis_size(axis)
        if count & (count - 1):
            values = lax.psum(values, axis)
            continue
        stride = 1
        while stride < count:
            values = values + lax.ppermute(values, axis, [(i, i ^ stride) for i in range(count)])
            stride *= 2
    return values


SWEEPS = 3
RELAXATION = 0.8
TIME_STEP = 0.1


def make_nb(roll):
    def nb(x, dr, dc):
        if dr:
            x = roll(x, (-dr) % x.shape[0], 0)
        if dc:
            x = roll(x, (-dc) % x.shape[1], 1)
        return x

    return nb


def edges(nb, u, v, h, cov, dr, dc):
    du = nb(u, dr, dc) - u
    dv = nb(v, dr, dc) - v
    s = du * du + dv * dv
    p = jnp.exp(jnp.log(1.0 + s) * (-1.0 / 3.0))
    a = 0.5 * (h + nb(h, dr, dc)) * cov * nb(cov, dr, dc)
    return du, dv, s, p, a, a * p


def sweep_terms(nb, u, v, h, cov, fric, fu, fv):
    de = edges(nb, u, v, h, cov, 0, 1)
    ds = edges(nb, u, v, h, cov, 1, 0)
    ce, cs = de[5], ds[5]
    fe_u, fe_v = ce * de[0], ce * de[1]
    fs_u, fs_v = cs * ds[0], cs * ds[1]
    flux_u = fe_u + fs_u - nb(fe_u, 0, -1) - nb(fs_u, -1, 0)
    flux_v = fe_v + fs_v - nb(fe_v, 0, -1) - nb(fs_v, -1, 0)
    c_sum = ce + cs + nb(ce, 0, -1) + nb(cs, -1, 0)
    r_u = fu - fric * u + flux_u
    r_v = fv - fric * v + flux_v
    d = 1.0 + fric + c_sum
    return de, ds, r_u, r_v, d


def sweep_fwd(nb, u, v, h, cov, fric, fu, fv):
    de, ds, r_u, r_v, d = sweep_terms(nb, u, v, h, cov, fric, fu, fv)
    return cov * (u + RELAXATION * r_u / d), cov * (v + RELAXATION * r_v / d)


def sweep_bwd(nb, u, v, h, cov, fric, su, sv, bu, bv):
    de, ds, r_u, r_v, d = sweep_terms(nb, u, v, h, cov, fric, h * su, h * sv)
    qu, qv = cov * bu, cov * bv
    tu, tv = RELAXATION * qu / d, RELAXATION * qv / d
    d_bar = -(tu * r_u + tv * r_v) / d
    f_bar = d_bar - (tu * u + tv * v)
    h_bar = tu * su + tv * sv
    wu = qu - fric * tu
    wv = qv - fric * tv
    for (du, dv, s, p, a, c), (dr, dc) in ((de, (0, 1)), (ds, (1, 0))):
        big_u = tu - nb(tu, dr, dc)
        big_v = tv - nb(tv, dr, dc)
        c_bar = big_u * du + big_v * dv + d_bar + nb(d_bar, dr, dc)
        a_bar = c_bar * p
        s_bar = c_bar * a * (-1.0 / 3.0) * p / (1.0 + s)
        gu = big_u * c + 2.0 * s_bar * du
        gv = big_v * c + 2.0 * s_bar * dv
        wu = wu - gu + nb(gu, -dr, -dc)
        wv = wv - gv + nb(gv, -dr, -dc)
        k = 0.5 * cov * nb(cov, dr, dc) * a_bar
        h_bar = h_bar + k + nb(k, -dr, -dc)
    return wu, wv, h_bar, f_bar


def transport_bwd(nb, u, v, h, cov, don_e, don_s, g):
    q = cov * g
    h_bar = q
    div_bar = -TIME_STEP * q
    u_bar = None
    v_bar = None
    for vel, don, (dr, dc) in ((u, don_e, (0, 1)), (v, don_s, (1, 0))):
        f_bar = div_bar - nb(div_bar, dr, dc)
        kk = cov * nb(cov, dr, dc)
        speed = 0.5 * (vel + nb(vel, dr, dc))
        hh = don * h + (1.0 - don) * nb(h, dr, dc)
        x = 0.5 * f_bar * kk * hh
        vb = x + nb(x, -dr, -dc)
        y = f_bar * speed * kk
        h_bar = h_bar + y * don + nb(y * (1.0 - don), -dr, -dc)
        if u_bar is None:
            u_bar = vb
        else:
            v_bar = vb
    return u_bar, v_bar, h_bar


def statics(f):
    mask = f["mask"]
    cov = (mask > 0.5).astype(jnp.float32)
    grounded = (mask > 1.5).astype(jnp.float32)
    flags = f["flags"]
    don_s = (flags > 1.5).astype(jnp.float32)
    don_e = flags - 2.0 * don_s
    fric = f["beta"] * grounded
    return cov, grounded, don_e, don_s, fric


def forward_all(nb, f, steps):
    cov, grounded, don_e, don_s, fric = statics(f)
    out = []
    for n in range(steps):
        h = f["thick"][n]
        u, v = f["vel"][n]
        fu, fv = h * f["slope"][0], h * f["slope"][1]
        for _ in range(SWEEPS):
            u, v = sweep_fwd(nb, u, v, h, cov, fric, fu, fv)
        out.append((u, v))
    return out


def backward_all(nb, f, steps, scales, g):
    cov, grounded, don_e, don_s, fric = statics(f)
    su, sv = f["slope"][0], f["slope"][1]
    beta = jnp.zeros_like(g)
    for n in reversed(range(steps)):
        h = f["thick"][n]
        u, v = f["vel"][n]
        fu, fv = h * su, h * sv
        states = []
        for _ in range(SWEEPS):
            states.append((u, v))
            u, v = sweep_fwd(nb, u, v, h, cov, fric, fu, fv)
        ou, ov = f["obs"][n]
        inv = 1.0 / scales[n]
        bu, bv, h_bar = transport_bwd(nb, u, v, h, cov, don_e, don_s, g)
        bu = bu + grounded * (u - ou) * inv
        bv = bv + grounded * (v - ov) * inv
        f_tot = jnp.zeros_like(g)
        for k in reversed(range(SWEEPS)):
            wu, wv = states[k]
            bu, bv, hb, fb = sweep_bwd(nb, wu, wv, h, cov, fric, su, sv, bu, bv)
            h_bar = h_bar + hb
            f_tot = f_tot + fb
        beta = beta + grounded * f_tot
        g = h_bar
    return beta, g


def unpack(arr, steps):
    return {
        "mask": arr[0],
        "flags": arr[1],
        "beta": arr[2],
        "slope": (arr[3], arr[4]),
        "thick": [arr[5 + n] for n in range(steps)],
        "vel": [(arr[5 + steps + 2 * n], arr[6 + steps + 2 * n]) for n in range(steps)],
        "obs": [(arr[5 + 3 * steps + 2 * n], arr[6 + 3 * steps + 2 * n]) for n in range(steps)],
        "adj": arr[5 + 5 * steps],
    }


class RefLoader:
    def __init__(self, ref, steps):
        self.ref = ref
        self.steps = steps

    def __getitem__(self, key):
        r, steps = self.ref, self.steps
        if key == "mask":
            return r[0]
        if key == "flags":
            return r[1]
        if key == "beta":
            return r[2]
        if key == "slope":
            return (r[3], r[4])
        if key == "thick":
            return [r[5 + n] for n in range(steps)]
        if key == "vel":
            return [(r[5 + steps + 2 * n], r[6 + steps + 2 * n]) for n in range(steps)]
        if key == "obs":
            return [(r[5 + 3 * steps + 2 * n], r[6 + 3 * steps + 2 * n]) for n in range(steps)]
        if key == "adj":
            return r[5 + 5 * steps]
        raise KeyError(key)


def forward_kernel(steps, rows, cols):
    def kernel(f_ref, o_ref):
        nb = make_nb(pltpu.roll)
        loader = RefLoader(f_ref, steps)
        out = forward_all(nb, loader, steps)
        grounded = (loader["mask"][:rows, :cols] > 1.5).astype(jnp.float32)

        def total(x):
            return jnp.sum(x)

        for n, (u, v) in enumerate(out):
            ou, ov = loader["obs"][n]
            ou, ov = ou[:rows, :cols], ov[:rows, :cols]
            du, dv = u[:rows, :cols] - ou, v[:rows, :cols] - ov
            o_ref[n] = total(grounded * (ou * ou + ov * ov))
            o_ref[steps + n] = total(0.5 * grounded * (du * du + dv * dv))

    return kernel


def backward_kernel(steps, rows, cols, cell_count):
    def kernel(s_ref, f_ref, beta_ref, g_ref, m_ref):
        nb = make_nb(pltpu.roll)
        loader = RefLoader(f_ref, steps)
        scales = [s_ref[n] / cell_count + EPSILON for n in range(steps)]
        misfit = s_ref[2 * steps - 1] / cell_count / scales[steps - 1]
        for n in reversed(range(steps - 1)):
            misfit = misfit + s_ref[steps + n] / cell_count / scales[n]
        m_ref[0] = misfit
        beta, g = backward_all(nb, loader, steps, scales, loader["adj"])
        beta_ref[...] = beta[:rows, :cols]
        g_ref[...] = g[:rows, :cols]

    return kernel


def pack_kernel(steps):
    def kernel(thick_ref, vel_ref, slope_ref, beta_ref, mask_ref, flags_ref, obs_ref, adj_ref, o_ref, top_ref, bottom_ref):
        f32 = jnp.float32
        o_ref[0] = mask_ref[...].astype(f32)
        o_ref[1] = flags_ref[...].astype(f32)
        o_ref[2] = beta_ref[...]
        for c in range(2):
            o_ref[3 + c] = slope_ref[c].astype(f32)
        for n in range(steps):
            o_ref[5 + n] = thick_ref[n].astype(f32)
            for c in range(2):
                o_ref[5 + steps + 2 * n + c] = vel_ref[n, c].astype(f32)
                o_ref[5 + 3 * steps + 2 * n + c] = obs_ref[n, c].astype(f32)
        o_ref[5 + 5 * steps] = adj_ref[...]
        width = top_ref.shape[1]
        top_ref[...] = o_ref[:, :width, :]
        bottom_ref[...] = o_ref[:, o_ref.shape[1] - width :, :]

    return kernel


def run_pack(width, *arrays):
    steps, rows, cols = arrays[0].shape
    fields = 6 + 5 * steps
    return pl.pallas_call(
        pack_kernel(steps),
        out_shape=(
            jax.ShapeDtypeStruct((fields, rows, cols), jnp.float32),
            jax.ShapeDtypeStruct((fields, width, cols), jnp.float32),
            jax.ShapeDtypeStruct((fields, width, cols), jnp.float32),
        ),
        in_specs=[pl.BlockSpec(memory_space=pltpu.VMEM)] * len(arrays),
        out_specs=(pl.BlockSpec(memory_space=pltpu.VMEM),) * 3,
    )(*arrays)


def run_forward(fields, steps, rows, cols):
    return pl.pallas_call(
        forward_kernel(steps, rows, cols),
        out_shape=jax.ShapeDtypeStruct((2 * steps,), jnp.float32),
        in_specs=[pl.BlockSpec(memory_space=pltpu.VMEM)],
        out_specs=pl.BlockSpec(memory_space=pltpu.SMEM),
    )(fields)


def run_backward(totals, fields, steps, rows, cols, cell_count):
    return pl.pallas_call(
        backward_kernel(steps, rows, cols, cell_count),
        out_shape=(jax.ShapeDtypeStruct((rows, cols), jnp.float32),) * 2
        + (jax.ShapeDtypeStruct((1,), jnp.float32),),
        in_specs=[pl.BlockSpec(memory_space=pltpu.SMEM), pl.BlockSpec(memory_space=pltpu.VMEM)],
        out_specs=(pl.BlockSpec(memory_space=pltpu.VMEM),) * 2 + (pl.BlockSpec(memory_space=pltpu.SMEM),),
    )(totals, fields)


def on_device(
    saved_thickness,
    saved_velocity,
    surface_slope,
    basal_beta,
    cell_mask,
    upwind_flags,
    observed_velocity,
    thickness_adjoint,
):
    steps = saved_thickness.shape[0]
    rows, cols = basal_beta.shape
    f32 = jnp.float32
    fields, first_rows, last_rows = run_pack(
        HALO,
        saved_thickness,
        saved_velocity,
        surface_slope,
        basal_beta,
        cell_mask,
        upwind_flags,
        observed_velocity,
        thickness_adjoint,
    )
    wide = wrapped_patch(fields, HALO, first_rows, last_rows)
    local_sums = run_forward(wide, steps, rows, cols)
    totals = butterfly_sum(local_sums, ("gx", "gy"))
    cell_count = rows * cols * lax.axis_size("gy") * lax.axis_size("gx")
    beta_gradient, thickness_gradient, misfit = run_backward(totals, wide, steps, rows, cols, cell_count)
    return (beta_gradient, thickness_gradient, misfit.reshape(()))


def solution(mesh):
    in_specs = (
        P(None, "gy", "gx"),
        P(None, None, "gy", "gx"),
        P(None, "gy", "gx"),
        P("gy", "gx"),
        P("gy", "gx"),
        P("gy", "gx"),
        P(None, None, "gy", "gx"),
        P("gy", "gx"),
    )
    out_specs = (P("gy", "gx"), P("gy", "gx"), P())
    return jax.shard_map(
        on_device, mesh=mesh, in_specs=in_specs, out_specs=out_specs, check_vma=False
    )
```
